32 devices in a mesh: section: 2 (over x), fsdp: 16 (over z, y, core).
Axes of the slice: x: 2, y: 2, z: 4, core: 2. Of those that a mesh axis runs over, the one named last changes fastest.
Arguments:
- history: bfloat16 [4, 16, 32, 2048], P(None, 'fsdp'), may hold values from -6 to 6
- keymask: int32 [4, 16, 32], P(None, 'fsdp'), may hold values from 0 to 1, as said below
- codes: int32 [4, 16, 16, 2], P(None, 'fsdp'), may hold values from 0 to 15
- plan_table: bfloat16 [16, 2048], replicated, may hold values from -6 to 6
- query_weights: bfloat16 [2, 2048, 1024], P('section', 'fsdp'), may hold values from -0.125 to 0.125
- output_weights: bfloat16 [2, 1024, 2048], P('section', 'fsdp'), may hold values from -0.75 to 0.75
- gains: float32 [2, 2048], P('section'), may hold values from 0.5 to 1.5
- cotangent: bfloat16 [4, 16, 32, 2048], P(None, 'fsdp'), may hold values from -6 to 6
Outputs:
- section_grads: bfloat16 [2, 4, 16, 32, 2048], P('section', None, 'fsdp')
- gain_grads: float32 [2, 2048], P('section')
The draws below stay inside these ranges and needn't reach their ends.
Inputs may be any that keep to these rules, and one draw needn't show every extreme that they name: `keymask`: in each series the ones form one run that ends at the last position and covers at least a quarter of the 32 positions.
All inputs are finite; a program needn't handle non-finite values.
Results may differ from the reference program's by a relative error of at most 0.014.
Values may be sent and summed in bfloat16 or wider, within the bound.
No kernel may reach another device: no remote copies, remote signals or barrier semaphores. Data moves between devices by JAX's collectives and lax.ppermute only.
A program may use at most 64 MiB of HBM per device.

```python
import math
import jax
import jax.numpy as jnp
from jax import lax

D = 2048
HEADS = 8
PLANS = 16
NCODE = 16
MB = 4
LEN = 32
HZ = 2
VW = 1024
SERIES = 16
SECTIONS = 2
N_SECTION = 2


def draw_keymask(key, part):
    observed = jax.random.randint(key, (MB, SERIES), LEN // 4, LEN + 1)
    position = jnp.arange(LEN, dtype=jnp.int32)
    return (position[None, None, :] >= LEN - observed[:, :, None]).astype(jnp.int32)


def plant(result, rng, least, top_value):
    shape = result.shape
    spot = [jax.random.randint(jax.random.fold_in(rng, axis), (), 0, shape[axis]) for axis in range(len(shape))]
    result = result.at[tuple(spot)].set(least)
    longest = shape.index(max(shape))
    spot[longest] = (spot[longest] + 1) % shape[longest]
    return result.at[tuple(spot)].set(top_value)


def strengthened(values, own_key, source, target, shards_of, factor):
    def block_of(dim):
        return (jnp.arange(values.shape[dim]) // (values.shape[dim] // shards_of)).reshape((-1,) + (1,) * (values.ndim - 1 - dim))

    one_side = jax.random.permutation(own_key, shards_of)[block_of(target)]
    other_side = (block_of(target) + shards_of // 2) % shards_of
    return jnp.where((block_of(source) == one_side) | (block_of(source) == other_side), factor * values, values)


def block_scale(rng, shape, shards, low, high):
    loudness, own = 1.0, jax.random.fold_in(rng, 6)
    for axis_at, shards_of in shards:
        draws = jnp.exp(jax.random.uniform(jax.random.fold_in(own, axis_at), (shards_of,), jnp.float32, low / len(shards), high / len(shards)))
        loudness = loudness * jnp.repeat(draws, shape[axis_at] // shards_of).reshape([-1 if axis == axis_at else 1 for axis in range(len(shape))])
    return loudness


def bell_draw(stream_key, extent, scale, most, cuts=(), kind=jnp.bfloat16):
    entries = scale * jax.random.normal(stream_key, extent, jnp.float32)
    if cuts:
        entries = entries * block_scale(stream_key, extent, cuts, -0.22, 0.18)
    return jnp.clip(entries, -most, most).astype(kind)


def heavy_noise(own_key, extent, spread, reach, split, heavy, held_as=jnp.bfloat16):
    values = spread * jax.random.normal(own_key, extent, jnp.float32)
    if split:
        values = values * block_scale(own_key, extent, split, -0.22, 0.18)
    return jnp.clip(strengthened(values, jax.random.fold_in(own_key, 3), *heavy), -reach, reach).astype(held_as)


def setup_inputs(seed: int = 0) -> dict:
    keys = jax.random.split(jax.random.key(seed), 9)
    history = bell_draw(keys[0], (MB, SERIES, LEN, D), 1.0, 6.0, ((1, 16),))
    keymask = draw_keymask(jax.random.fold_in(keys[8], 71), 0)
    codes = plant(jax.random.randint(keys[2], (MB, SERIES, PLANS, HZ), 0, NCODE), jax.random.fold_in(keys[2], 1), 0, NCODE - 1).astype(jnp.int32)
    plan_table = bell_draw(keys[3], (NCODE, D), 1.0, 6.0)
    query_weights = bell_draw(keys[4], (SECTIONS, D, VW), D ** -0.5, 0.125, ((0, 2), (1, 16)))
    output_weights = bell_draw(keys[5], (SECTIONS, VW, D), (VW // 16) ** -0.5, 0.75, ((0, 2), (1, 16)))
    gains = jnp.clip(1.0 + 0.1 * jax.random.normal(keys[6], (SECTIONS, D), jnp.float32), 0.5, 1.5)
    cotangent = heavy_noise(keys[7], (MB, SERIES, LEN, D), 1.0, 6.0, ((1, 16),), (1, 3, 16, 2.0))
    return {"history": history, "keymask": keymask, "codes": codes, "plan_table": plan_table, "query_weights": query_weights, "output_weights": output_weights, "gains": gains, "cotangent": cotangent}


EPSILON = 1e-05

def rms_scale(inputs, gain_vector):
    return inputs * lax.rsqrt(lax.optimization_barrier(jnp.mean(inputs * inputs, axis=-1, keepdims=True)) + EPSILON) * gain_vector

def to_half(inputs):
    return lax.optimization_barrier(inputs.astype(jnp.bfloat16)).astype(jnp.float32)

def attend_layer(section_input, source, key_mask, query_weight, output_weight, gain_vector):
    batch_size, seq_length, model_width = section_input.shape
    half_width = model_width // 2
    head_dim = half_width // HEADS
    head_shape = (batch_size, seq_length, HEADS, head_dim)
    input_wide = section_input.astype(jnp.float32)
    normed = rms_scale(input_wide, gain_vector)
    normed_source = rms_scale(source.astype(jnp.float32), gain_vector)
    normed_rows = normed.astype(jnp.bfloat16).reshape(batch_size * seq_length, model_width)
    query_flat = jnp.dot(normed_rows, query_weight, preferred_element_type=jnp.float32)
    queries = to_half(query_flat).reshape(head_shape)
    key_rows = to_half(normed_source[..., :half_width]).reshape(head_shape)
    value_rows = to_half(normed_source[..., half_width:]).reshape(head_shape)
    scores = jnp.einsum('bqhd,bkhd->bhqk', queries, key_rows) / math.sqrt(head_dim)
    raised = jnp.exp(scores) * key_mask.astype(jnp.float32)[:, None, None, :]
    probs = to_half(raised / lax.optimization_barrier(jnp.sum(raised, axis=-1, keepdims=True)))
    mixed = jnp.einsum('bhqk,bkhd->bqhd', probs, value_rows).astype(jnp.bfloat16)
    mixed = mixed.reshape(batch_size * seq_length, half_width)
    update = jnp.dot(mixed, output_weight, preferred_element_type=jnp.float32)
    return (input_wide + update.reshape(batch_size, seq_length, model_width)).astype(jnp.bfloat16)

def reference(history, keymask, codes, plan_table, query_weights, output_weights, gains, cotangent):
    half_sections = N_SECTION // 2
    plan_rows = codes.reshape(MB, SERIES, LEN)
    plan_tokens = plan_table[plan_rows]

    def forward(gain_all, probes):
        results = []
        for micro in range(MB):
            key_mask = keymask[micro]
            current = history[micro]
            for layer_index in range(half_sections):
                current = current + probes[layer_index, micro]
                current = attend_layer(current, current, key_mask, query_weights[layer_index], output_weights[layer_index], gain_all[layer_index])
            memory = current
            current = plan_tokens[micro]
            for layer_index in range(half_sections, N_SECTION):
                current = current + probes[layer_index, micro]
                current = attend_layer(current, memory, key_mask, query_weights[layer_index], output_weights[layer_index], gain_all[layer_index])
            results.append(current)
        return jnp.stack(results)
    probes = jnp.zeros((N_SECTION, MB, SERIES, LEN, D), jnp.bfloat16)
    _, pull = jax.vjp(forward, gains, probes)
    gain_grads, section_grads = pull(cotangent)
    return (section_grads, gain_grads)
```

```python
import math

import jax
import jax.numpy as jnp
from jax import lax
from jax.sharding import PartitionSpec as P

HEADS = 8


EPSILON = 1e-05


def send_to(arrays, axis, source, target):
    return lax.ppermute(arrays, axis, [(source, target)])


def rms_scale(inputs, gain_vector):
    return (
        inputs
        * lax.rsqrt(jnp.mean(inputs * inputs, axis=-1, keepdims=True) + EPSILON)
        * gain_vector
    )


def attend_layer(section_input, source, key_mask, query_weight, output_weight, gain_vector):
    series_count, seq_length, model_width = section_input.shape
    half_width = model_width // 2
    head_dim = half_width // HEADS
    head_shape = (series_count, seq_length, HEADS, head_dim)
    input_wide = section_input.astype(jnp.float32)
    normed = rms_scale(input_wide, gain_vector)
    normed_source = rms_scale(source.astype(jnp.float32), gain_vector)
    normed_rows = normed.astype(jnp.bfloat16).reshape(series_count * seq_length, model_width)
    query_flat = jnp.dot(normed_rows, query_weight, preferred_element_type=jnp.float32)
    queries = query_flat.astype(jnp.bfloat16).reshape(head_shape)
    key_rows = normed_source[..., :half_width].astype(jnp.bfloat16).reshape(head_shape)
    value_rows = normed_source[..., half_width:].astype(jnp.bfloat16).reshape(head_shape)
    scores = jnp.einsum(
        "bqhd,bkhd->bhqk", queries, key_rows, preferred_element_type=jnp.float32
    ) / math.sqrt(head_dim)
    raised = jnp.exp(scores) * key_mask.astype(jnp.float32)[:, None, None, :]
    probs = (raised / jnp.sum(raised, axis=-1, keepdims=True)).astype(jnp.bfloat16)
    mixed = jnp.einsum("bhqk,bkhd->bqhd", probs, value_rows, preferred_element_type=jnp.float32)
    mixed = mixed.astype(jnp.bfloat16).reshape(series_count * seq_length, half_width)
    update = jnp.dot(mixed, output_weight, preferred_element_type=jnp.float32)
    return (input_wide + update.reshape(series_count, seq_length, model_width)).astype(jnp.bfloat16)


def on_device(history, keymask, codes, plan_table, query_weights, output_weights, gains, cotangent):
    section_index = lax.axis_index("section")
    section_count = lax.axis_size("section")
    half_sections = section_count // 2
    micro_count, series_count, seq_length, model_width = history.shape
    rows = micro_count * series_count
    act_shape = (rows, seq_length, model_width)
    query_weight = lax.all_gather(query_weights, "fsdp", axis=1, tiled=True)[0]
    output_weight = lax.all_gather(output_weights, "fsdp", axis=1, tiled=True)[0]
    gain_vector = gains[0]
    code_rows = codes.reshape(micro_count, series_count, seq_length)
    code_count = plan_table.shape[0]
    one_hot = (code_rows[..., None] == jnp.arange(code_count, dtype=jnp.int32)).astype(jnp.bfloat16)
    plan_tokens = jnp.einsum(
        "msln,nd->msld", one_hot, plan_table, preferred_element_type=jnp.float32
    ).astype(jnp.bfloat16).reshape(act_shape)
    key_mask = keymask.reshape(rows, seq_length)
    history_rows = history.reshape(act_shape)

    def encoder_map(layer_input, layer_gain):
        return attend_layer(
            layer_input, layer_input, key_mask, query_weight, output_weight, layer_gain
        )

    def decoder_map(layer_input, layer_memory, layer_gain):
        return attend_layer(
            layer_input, layer_memory, key_mask, query_weight, output_weight, layer_gain
        )

    saved_inputs = {}
    got_input = None
    got_memory = None
    for tick in range(section_count - 1):
        if tick == 0:
            layer_input = history_rows
        elif tick == half_sections:
            layer_input = plan_tokens
        else:
            layer_input = got_input
        if tick < half_sections:
            output = encoder_map(layer_input, gain_vector)
            saved_inputs[tick] = (layer_input, None)
            if tick == half_sections - 1:
                got_memory = send_to(output, "section", tick, tick + 1)
            else:
                got_input = send_to(output, "section", tick, tick + 1)
        else:
            output = decoder_map(layer_input, got_memory, gain_vector)
            saved_inputs[tick] = (layer_input, got_memory)
            got_input, got_memory = send_to((output, got_memory), "section", tick, tick + 1)
    last = section_count - 1
    if last == half_sections:
        saved_inputs[last] = (plan_tokens, got_memory)
    else:
        saved_inputs[last] = (got_input, got_memory)

    zero_gain = jnp.zeros_like(gain_vector)
    grads_out = jnp.zeros(act_shape, jnp.bfloat16)
    gain_total = zero_gain
    got_grad = None
    got_memory_grad = None
    for tick in range(section_count):
        run = section_count - 1 - tick
        out_grad = cotangent.reshape(act_shape) if run == section_count - 1 else got_grad
        layer_input, layer_memory = saved_inputs[run]
        mine = section_index == run
        if run >= half_sections:
            _, pull = jax.vjp(decoder_map, layer_input, layer_memory, gain_vector)
            input_grad, memory_grad, gain_grad = pull(out_grad)
            if got_memory_grad is not None:
                memory_grad = got_memory_grad + memory_grad
            if run == half_sections:
                got_grad = send_to(memory_grad, "section", run, run - 1)
            else:
                got_grad, got_memory_grad = send_to(
                    (input_grad, memory_grad), "section", run, run - 1
                )
        else:
            _, pull = jax.vjp(encoder_map, layer_input, gain_vector)
            input_grad, gain_grad = pull(out_grad)
            if run > 0:
                got_grad = send_to(input_grad, "section", run, run - 1)
        grads_out = jnp.where(mine, input_grad, grads_out)
        gain_total = gain_total + jnp.where(mine, gain_grad, zero_gain)
    gain_total = lax.psum(gain_total, "fsdp")
    grads_out = grads_out.reshape(history.shape)
    return (grads_out[None], gain_total[None])


def solution(mesh):
    return jax.shard_map(
        on_device,
        mesh=mesh,
        in_specs=(
            P(None, "fsdp", None, None),
            P(None, "fsdp", None),
            P(None, "fsdp", None, None),
            P(),
            P("section", "fsdp", None),
            P("section", "fsdp", None),
            P("section", None),
            P(None, "fsdp", None, None),
        ),
        out_specs=(P("section", None, "fsdp", None, None), P("section", None)),
        check_vma=False,
    )
```

```python
import math

import jax
import jax.numpy as jnp
from jax import lax
from jax.sharding import PartitionSpec as P

HEADS = 8


EPSILON = 1e-05


def send_to(arrays, axis, source, target):
    return lax.ppermute(arrays, axis, [(source, target)])


def butterfly_gather(shard, axis, size):
    if size & (size - 1):
        return lax.all_gather(shard, axis, axis=1, tiled=True)[0]
    index = lax.axis_index(axis)
    held = shard
    step = size // 2
    while step >= 1:
        other = lax.ppermute(held, axis, [(j, j ^ step) for j in range(size)])
        held = jnp.concatenate([held, other], axis=0)
        step //= 2
    bits = size.bit_length() - 1

    def reversed_bits(value):
        total = 0
        for bit in range(bits):
            total = total + ((value >> bit) & 1) * (1 << (bits - 1 - bit))
        return total

    flipped = reversed_bits(index)
    blocks = [
        lax.dynamic_index_in_dim(held, flipped ^ reversed_bits(j), 0, False) for j in range(size)
    ]
    return jnp.concatenate(blocks, axis=0)


def butterfly_sum(value, axis, size):
    if size & (size - 1):
        return lax.psum(value, axis)
    step = 1
    while step < size:
        value = value + lax.ppermute(value, axis, [(j, j ^ step) for j in range(size)])
        step *= 2
    return value


def rms_scale(inputs, gain_vector):
    return (
        inputs
        * lax.rsqrt(jnp.mean(inputs * inputs, axis=-1, keepdims=True) + EPSILON)
        * gain_vector
    )


def attend_layer(section_input, source, key_mask, query_weight, output_weight, gain_vector):
    series_count, seq_length, model_width = section_input.shape
    half_width = model_width // 2
    head_dim = half_width // HEADS
    head_shape = (series_count, seq_length, HEADS, head_dim)
    input_wide = section_input.astype(jnp.float32)
    normed = rms_scale(input_wide, gain_vector)
    normed_source = rms_scale(source.astype(jnp.float32), gain_vector)
    normed_rows = normed.astype(jnp.bfloat16).reshape(series_count * seq_length, model_width)
    query_flat = jnp.dot(normed_rows, query_weight, preferred_element_type=jnp.float32)
    queries = query_flat.astype(jnp.bfloat16).reshape(head_shape)
    key_rows = normed_source[..., :half_width].astype(jnp.bfloat16).reshape(head_shape)
    value_rows = normed_source[..., half_width:].astype(jnp.bfloat16).reshape(head_shape)
    scores = jnp.einsum(
        "bqhd,bkhd->bhqk", queries, key_rows, preferred_element_type=jnp.float32
    ) / math.sqrt(head_dim)
    raised = jnp.exp(scores) * key_mask.astype(jnp.float32)[:, None, None, :]
    probs = (raised / jnp.sum(raised, axis=-1, keepdims=True)).astype(jnp.bfloat16)
    mixed = jnp.einsum("bhqk,bkhd->bqhd", probs, value_rows, preferred_element_type=jnp.float32)
    mixed = mixed.astype(jnp.bfloat16).reshape(series_count * seq_length, half_width)
    update = jnp.dot(mixed, output_weight, preferred_element_type=jnp.float32)
    return (input_wide + update.reshape(series_count, seq_length, model_width)).astype(jnp.bfloat16)


def on_device(history, keymask, codes, plan_table, query_weights, output_weights, gains, cotangent):
    section_index = lax.axis_index("section")
    section_count = lax.axis_size("section")
    half_sections = section_count // 2
    micro_count, series_count, seq_length, model_width = history.shape
    rows = micro_count * series_count
    act_shape = (rows, seq_length, model_width)
    query_weight = lax.all_gather(query_weights, "fsdp", axis=1, tiled=True)[0]
    fsdp_count = lax.axis_size("fsdp")
    output_weight = butterfly_gather(output_weights, "fsdp", fsdp_count)
    gain_vector = gains[0]
    code_rows = codes.reshape(micro_count, series_count, seq_length)
    code_count = plan_table.shape[0]
    one_hot = (code_rows[..., None] == jnp.arange(code_count, dtype=jnp.int32)).astype(jnp.bfloat16)
    plan_tokens = jnp.einsum(
        "msln,nd->msld", one_hot, plan_table, preferred_element_type=jnp.float32
    ).astype(jnp.bfloat16).reshape(act_shape)
    key_mask = keymask.reshape(rows, seq_length)
    history_rows = history.reshape(act_shape)

    def encoder_map(layer_input, layer_gain):
        return attend_layer(
            layer_input, layer_input, key_mask, query_weight, output_weight, layer_gain
        )

    def decoder_map(layer_input, layer_memory, layer_gain):
        return attend_layer(
            layer_input, layer_memory, key_mask, query_weight, output_weight, layer_gain
        )

    saved_inputs = {}
    got_input = None
    got_memory = None
    for tick in range(section_count - 1):
        if tick == 0:
            layer_input = history_rows
        elif tick == half_sections:
            layer_input = plan_tokens
        else:
            layer_input = got_input
        if tick < half_sections:
            output = encoder_map(layer_input, gain_vector)
            saved_inputs[tick] = (layer_input, None)
            if tick == half_sections - 1:
                got_memory = send_to(output, "section", tick, tick + 1)
            else:
                got_input = send_to(output, "section", tick, tick + 1)
        else:
            output = decoder_map(layer_input, got_memory, gain_vector)
            saved_inputs[tick] = (layer_input, got_memory)
            got_input, got_memory = send_to((output, got_memory), "section", tick, tick + 1)
    last = section_count - 1
    if last == half_sections:
        saved_inputs[last] = (plan_tokens, got_memory)
    else:
        saved_inputs[last] = (got_input, got_memory)

    zero_gain = jnp.zeros_like(gain_vector)
    grads_out = jnp.zeros(act_shape, jnp.bfloat16)
    gain_total = zero_gain
    got_grad = None
    got_memory_grad = None
    for tick in range(section_count):
        run = section_count - 1 - tick
        out_grad = cotangent.reshape(act_shape) if run == section_count - 1 else got_grad
        layer_input, layer_memory = saved_inputs[run]
        mine = section_index == run
        if run >= half_sections:
            _, pull = jax.vjp(decoder_map, layer_input, layer_memory, gain_vector)
            input_grad, memory_grad, gain_grad = pull(out_grad)
            if got_memory_grad is not None:
                memory_grad = got_memory_grad + memory_grad
            if run == half_sections:
                got_grad = send_to(memory_grad, "section", run, run - 1)
            else:
                got_grad, got_memory_grad = send_to(
                    (input_grad, memory_grad), "section", run, run - 1
                )
        else:
            _, pull = jax.vjp(encoder_map, layer_input, gain_vector)
            input_grad, gain_grad = pull(out_grad)
            if run > 0:
                got_grad = send_to(input_grad, "section", run, run - 1)
        grads_out = jnp.where(mine, input_grad, grads_out)
        gain_total = gain_total + jnp.where(mine, gain_grad, zero_gain)
    gain_total = butterfly_sum(gain_total, "fsdp", fsdp_count)
    grads_out = grads_out.reshape(history.shape)
    return (grads_out[None], gain_total[None])


def solution(mesh):
    return jax.shard_map(
        on_device,
        mesh=mesh,
        in_specs=(
            P(None, "fsdp", None, None),
            P(None, "fsdp", None),
            P(None, "fsdp", None, None),
            P(),
            P("section", "fsdp", None),
            P("section", "fsdp", None),
            P("section", None),
            P(None, "fsdp", None, None),
        ),
        out_specs=(P("section", None, "fsdp", None, None), P("section", None)),
        check_vma=False,
    )
```

```python
import math

import jax
import jax.numpy as jnp
from jax import lax
from jax.sharding import PartitionSpec as P

HEADS = 8


EPSILON = 1e-05


def send_to(arrays, axis, source, target):
    return lax.ppermute(arrays, axis, [(source, target)])


def exchange_orders(size):
    steps = []
    step = size // 2
    while step >= 1:
        steps.append(step)
        step //= 2
    other = list(steps)
    if len(other) >= 3:
        other[1], other[2] = other[2], other[1]
    return steps, other


def butterfly_gathers(shards, orders, axis, size):
    index = lax.axis_index(axis)
    held = [shard for shard in shards]
    for level in range(len(orders[0])):
        for which, order in enumerate(orders):
            step = order[level]
            other = lax.ppermute(held[which], axis, [(j, j ^ step) for j in range(size)])
            upper = ((index // step) % 2) == 1
            low = jnp.where(upper, other, held[which])
            high = jnp.where(upper, held[which], other)
            held[which] = jnp.stack([low, high], axis=1).reshape(
                (-1,) + held[which].shape[1:]
            )
    results = []
    for which, order in enumerate(orders):
        block_rows, width = held[which].shape[1:]
        wanted = sorted(order, reverse=True)
        if order != wanted:
            split = held[which].reshape(tuple(2 for _ in order) + (block_rows, width))
            axes = tuple(order.index(value) for value in wanted) + (len(order), len(order) + 1)
            held[which] = jnp.transpose(split, axes)
        results.append(held[which].reshape(size * block_rows, width))
    return results


def butterfly_sum(value, axis, size):
    if size & (size - 1):
        return lax.psum(value, axis)
    step = 1
    while step < size:
        value = value + lax.ppermute(value, axis, [(j, j ^ step) for j in range(size)])
        step *= 2
    return value


def rms_scale(inputs, gain_vector):
    return (
        inputs
        * lax.rsqrt(jnp.mean(inputs * inputs, axis=-1, keepdims=True) + EPSILON)
        * gain_vector
    )


def attend_layer(section_input, source, key_mask, query_weight, output_weight, gain_vector):
    series_count, seq_length, model_width = section_input.shape
    half_width = model_width // 2
    head_dim = half_width // HEADS
    head_shape = (series_count, seq_length, HEADS, head_dim)
    input_wide = section_input.astype(jnp.float32)
    normed = rms_scale(input_wide, gain_vector)
    normed_source = rms_scale(source.astype(jnp.float32), gain_vector)
    normed_rows = normed.astype(jnp.bfloat16).reshape(series_count * seq_length, model_width)
    query_flat = jnp.dot(normed_rows, query_weight, preferred_element_type=jnp.float32)
    queries = query_flat.astype(jnp.bfloat16).reshape(head_shape)
    key_rows = normed_source[..., :half_width].astype(jnp.bfloat16).reshape(head_shape)
    value_rows = normed_source[..., half_width:].astype(jnp.bfloat16).reshape(head_shape)
    scores = jnp.einsum(
        "bqhd,bkhd->bhqk", queries, key_rows, preferred_element_type=jnp.float32
    ) / math.sqrt(head_dim)
    raised = jnp.exp(scores) * key_mask.astype(jnp.float32)[:, None, None, :]
    probs = (raised / jnp.sum(raised, axis=-1, keepdims=True)).astype(jnp.bfloat16)
    mixed = jnp.einsum("bhqk,bkhd->bqhd", probs, value_rows, preferred_element_type=jnp.float32)
    mixed = mixed.astype(jnp.bfloat16).reshape(series_count * seq_length, half_width)
    update = jnp.dot(mixed, output_weight, preferred_element_type=jnp.float32)
    return (input_wide + update.reshape(series_count, seq_length, model_width)).astype(jnp.bfloat16)


def on_device(history, keymask, codes, plan_table, query_weights, output_weights, gains, cotangent):
    section_index = lax.axis_index("section")
    section_count = lax.axis_size("section")
    half_sections = section_count // 2
    micro_count, series_count, seq_length, model_width = history.shape
    rows = micro_count * series_count
    act_shape = (rows, seq_length, model_width)
    fsdp_count = lax.axis_size("fsdp")
    if fsdp_count & (fsdp_count - 1):
        query_weight = lax.all_gather(query_weights, "fsdp", axis=1, tiled=True)[0]
        output_weight = lax.all_gather(output_weights, "fsdp", axis=1, tiled=True)[0]
    else:
        query_weight, output_weight = butterfly_gathers(
            [query_weights, output_weights], exchange_orders(fsdp_count), "fsdp", fsdp_count
        )
    gain_vector = gains[0]
    code_rows = codes.reshape(micro_count, series_count, seq_length)
    code_count = plan_table.shape[0]
    one_hot = (code_rows[..., None] == jnp.arange(code_count, dtype=jnp.int32)).astype(jnp.bfloat16)
    plan_tokens = jnp.einsum(
        "msln,nd->msld", one_hot, plan_table, preferred_element_type=jnp.float32
    ).astype(jnp.bfloat16).reshape(act_shape)
    key_mask = keymask.reshape(rows, seq_length)
    history_rows = history.reshape(act_shape)

    def encoder_map(layer_input, layer_gain):
        return attend_layer(
            layer_input, layer_input, key_mask, query_weight, output_weight, layer_gain
        )

    def decoder_map(layer_input, layer_memory, layer_gain):
        return attend_layer(
            layer_input, layer_memory, key_mask, query_weight, output_weight, layer_gain
        )

    saved_inputs = {}
    got_input = None
    got_memory = None
    for tick in range(section_count - 1):
        if tick == 0:
            layer_input = history_rows
        elif tick == half_sections:
            layer_input = plan_tokens
        else:
            layer_input = got_input
        if tick < half_sections:
            output = encoder_map(layer_input, gain_vector)
            saved_inputs[tick] = (layer_input, None)
            if tick == half_sections - 1:
                got_memory = send_to(output, "section", tick, tick + 1)
            else:
                got_input = send_to(output, "section", tick, tick + 1)
        else:
            output = decoder_map(layer_input, got_memory, gain_vector)
            saved_inputs[tick] = (layer_input, got_memory)
            got_input, got_memory = send_to((output, got_memory), "section", tick, tick + 1)
    last = section_count - 1
    if last == half_sections:
        saved_inputs[last] = (plan_tokens, got_memory)
    else:
        saved_inputs[last] = (got_input, got_memory)

    zero_gain = jnp.zeros_like(gain_vector)
    grads_out = jnp.zeros(act_shape, jnp.bfloat16)
    gain_total = zero_gain
    got_grad = None
    got_memory_grad = None
    for tick in range(section_count):
        run = section_count - 1 - tick
        out_grad = cotangent.reshape(act_shape) if run == section_count - 1 else got_grad
        layer_input, layer_memory = saved_inputs[run]
        mine = section_index == run
        if run >= half_sections:
            _, pull = jax.vjp(decoder_map, layer_input, layer_memory, gain_vector)
            input_grad, memory_grad, gain_grad = pull(out_grad)
            if got_memory_grad is not None:
                memory_grad = got_memory_grad + memory_grad
            if run == half_sections:
                got_grad = send_to(memory_grad, "section", run, run - 1)
            else:
                got_grad, got_memory_grad = send_to(
                    (input_grad, memory_grad), "section", run, run - 1
                )
        else:
            _, pull = jax.vjp(encoder_map, layer_input, gain_vector)
            input_grad, gain_grad = pull(out_grad)
            if run > 0:
                got_grad = send_to(input_grad, "section", run, run - 1)
        grads_out = jnp.where(mine, input_grad, grads_out)
        gain_total = gain_total + jnp.where(mine, gain_grad, zero_gain)
    gain_total = butterfly_sum(gain_total, "fsdp", fsdp_count)
    grads_out = grads_out.reshape(history.shape)
    return (grads_out[None], gain_total[None])


def solution(mesh):
    return jax.shard_map(
        on_device,
        mesh=mesh,
        in_specs=(
            P(None, "fsdp", None, None),
            P(None, "fsdp", None),
            P(None, "fsdp", None, None),
            P(),
            P("section", "fsdp", None),
            P("section", "fsdp", None),
            P("section", None),
            P(None, "fsdp", None, None),
        ),
        out_specs=(P("section", None, "fsdp", None, None), P("section", None)),
        check_vma=False,
    )
```

```python
import math

import jax
import jax.numpy as jnp
from jax import lax
from jax.sharding import PartitionSpec as P

HEADS = 8


EPSILON = 1e-05


def send_to(arrays, axis, source, target):
    return lax.ppermute(arrays, axis, [(source, target)])


def exchange_orders(size):
    steps = []
    step = size // 2
    while step >= 1:
        steps.append(step)
        step //= 2
    other = list(steps)
    if len(other) >= 3:
        other[1], other[2] = other[2], other[1]
    return steps, other


def butterfly_gathers(shards, orders, axis, size):
    index = lax.axis_index(axis)
    held = [shard for shard in shards]
    for level in range(len(orders[0])):
        for which, order in enumerate(orders):
            step = order[level]
            other = lax.ppermute(held[which], axis, [(j, j ^ step) for j in range(size)])
            upper = ((index // step) % 2) == 1
            low = jnp.where(upper, other, held[which])
            high = jnp.where(upper, held[which], other)
            held[which] = jnp.stack([low, high], axis=1).reshape(
                (-1,) + held[which].shape[1:]
            )
    results = []
    for which, order in enumerate(orders):
        block_rows, width = held[which].shape[1:]
        wanted = sorted(order, reverse=True)
        if order != wanted:
            split = held[which].reshape(tuple(2 for _ in order) + (block_rows, width))
            axes = tuple(order.index(value) for value in wanted) + (len(order), len(order) + 1)
            held[which] = jnp.transpose(split, axes)
        results.append(held[which].reshape(size * block_rows, width))
    return results


def spread_sum(value, axis, size):
    if size & (size - 1):
        return lax.psum(value, axis)
    index = lax.axis_index(axis)
    received = [value] + [
        lax.ppermute(value, axis, [(j, j ^ shift) for j in range(size)]) for shift in range(1, size)
    ]
    by_shift = jnp.stack(received, axis=0)
    by_source = jnp.take(by_shift, jnp.arange(size, dtype=jnp.int32) ^ index, axis=0)
    return jnp.sum(by_source, axis=0)


def rms_scale(inputs, gain_vector):
    return (
        inputs
        * lax.rsqrt(jnp.mean(inputs * inputs, axis=-1, keepdims=True) + EPSILON)
        * gain_vector
    )


def attend_layer(section_input, source, key_mask, query_weight, output_weight, gain_vector):
    series_count, seq_length, model_width = section_input.shape
    half_width = model_width // 2
    head_dim = half_width // HEADS
    head_shape = (series_count, seq_length, HEADS, head_dim)
    input_wide = section_input.astype(jnp.float32)
    normed = rms_scale(input_wide, gain_vector)
    normed_source = rms_scale(source.astype(jnp.float32), gain_vector)
    normed_rows = normed.astype(jnp.bfloat16).reshape(series_count * seq_length, model_width)
    query_flat = jnp.dot(normed_rows, query_weight, preferred_element_type=jnp.float32)
    queries = query_flat.astype(jnp.bfloat16).reshape(head_shape)
    key_rows = normed_source[..., :half_width].astype(jnp.bfloat16).reshape(head_shape)
    value_rows = normed_source[..., half_width:].astype(jnp.bfloat16).reshape(head_shape)
    scores = jnp.einsum(
        "bqhd,bkhd->bhqk", queries, key_rows, preferred_element_type=jnp.float32
    ) / math.sqrt(head_dim)
    raised = jnp.exp(scores) * key_mask.astype(jnp.float32)[:, None, None, :]
    probs = (raised / jnp.sum(raised, axis=-1, keepdims=True)).astype(jnp.bfloat16)
    mixed = jnp.einsum("bhqk,bkhd->bqhd", probs, value_rows, preferred_element_type=jnp.float32)
    mixed = mixed.astype(jnp.bfloat16).reshape(series_count * seq_length, half_width)
    update = jnp.dot(mixed, output_weight, preferred_element_type=jnp.float32)
    return (input_wide + update.reshape(series_count, seq_length, model_width)).astype(jnp.bfloat16)


def on_device(history, keymask, codes, plan_table, query_weights, output_weights, gains, cotangent):
    section_index = lax.axis_index("section")
    section_count = lax.axis_size("section")
    half_sections = section_count // 2
    micro_count, series_count, seq_length, model_width = history.shape
    rows = micro_count * series_count
    act_shape = (rows, seq_length, model_width)
    fsdp_count = lax.axis_size("fsdp")
    if fsdp_count & (fsdp_count - 1):
        query_weight = lax.all_gather(query_weights, "fsdp", axis=1, tiled=True)[0]
        output_weight = lax.all_gather(output_weights, "fsdp", axis=1, tiled=True)[0]
    else:
        query_weight, output_weight = butterfly_gathers(
            [query_weights, output_weights], exchange_orders(fsdp_count), "fsdp", fsdp_count
        )
    gain_vector = gains[0]
    code_rows = codes.reshape(micro_count, series_count, seq_length)
    code_count = plan_table.shape[0]
    one_hot = (code_rows[..., None] == jnp.arange(code_count, dtype=jnp.int32)).astype(jnp.bfloat16)
    plan_tokens = jnp.einsum(
        "msln,nd->msld", one_hot, plan_table, preferred_element_type=jnp.float32
    ).astype(jnp.bfloat16).reshape(act_shape)
    key_mask = keymask.reshape(rows, seq_length)
    history_rows = history.reshape(act_shape)

    def encoder_map(layer_input, layer_gain):
        return attend_layer(
            layer_input, layer_input, key_mask, query_weight, output_weight, layer_gain
        )

    def decoder_map(layer_input, layer_memory, layer_gain):
        return attend_layer(
            layer_input, layer_memory, key_mask, query_weight, output_weight, layer_gain
        )

    pullbacks = {}
    got_input = None
    got_memory = None
    for tick in range(section_count - 1):
        if tick == 0:
            layer_input = history_rows
        elif tick == half_sections:
            layer_input = plan_tokens
        else:
            layer_input = got_input
        if tick < half_sections:
            output, pull = jax.vjp(encoder_map, layer_input, gain_vector)
            pullbacks[tick] = pull
            if tick == half_sections - 1:
                got_memory = send_to(output, "section", tick, tick + 1)
            else:
                got_input = send_to(output, "section", tick, tick + 1)
        else:
            output, pull = jax.vjp(decoder_map, layer_input, got_memory, gain_vector)
            pullbacks[tick] = pull
            got_input, got_memory = send_to((output, got_memory), "section", tick, tick + 1)
    last = section_count - 1
    if last == half_sections:
        last_input = plan_tokens
    else:
        last_input = got_input
    pullbacks[last] = jax.vjp(decoder_map, last_input, got_memory, gain_vector)[1]

    zero_gain = jnp.zeros_like(gain_vector)
    grads_out = jnp.zeros(act_shape, jnp.bfloat16)
    gain_total = zero_gain
    got_grad = None
    got_memory_grad = None
    for tick in range(section_count):
        run = section_count - 1 - tick
        out_grad = cotangent.reshape(act_shape) if run == section_count - 1 else got_grad
        pull = pullbacks[run]
        mine = section_index == run
        if run >= half_sections:
            input_grad, memory_grad, gain_grad = pull(out_grad)
            if got_memory_grad is not None:
                memory_grad = got_memory_grad + memory_grad
            if run == half_sections:
                got_grad = send_to(memory_grad, "section", run, run - 1)
            else:
                got_grad, got_memory_grad = send_to(
                    (input_grad, memory_grad), "section", run, run - 1
                )
        else:
            input_grad, gain_grad = pull(out_grad)
            if run > 0:
                got_grad = send_to(input_grad, "section", run, run - 1)
        grads_out = jnp.where(mine, input_grad, grads_out)
        gain_total = gain_total + jnp.where(mine, gain_grad, zero_gain)
    gain_total = spread_sum(gain_total, "fsdp", fsdp_count)
    grads_out = grads_out.reshape(history.shape)
    return (grads_out[None], gain_total[None])


def solution(mesh):
    return jax.shard_map(
        on_device,
        mesh=mesh,
        in_specs=(
            P(None, "fsdp", None, None),
            P(None, "fsdp", None),
            P(None, "fsdp", None, None),
            P(),
            P("section", "fsdp", None),
            P("section", "fsdp", None),
            P("section", None),
            P(None, "fsdp", None, None),
        ),
        out_specs=(P("section", None, "fsdp", None, None), P("section", None)),
        check_vma=False,
    )
```

```python
import math

import jax
import jax.numpy as jnp
from jax import lax
from jax.sharding import PartitionSpec as P

HEADS = 8


EPSILON = 1e-05


def send_to(arrays, axis, source, target):
    return lax.ppermute(arrays, axis, [(source, target)])


def exchange_orders(size):
    steps = []
    step = size // 2
    while step >= 1:
        steps.append(step)
        step //= 2
    other = list(steps)
    if len(other) >= 3:
        other[1], other[2] = other[2], other[1]
    return steps, other


def butterfly_gathers(shards, orders, axis, size):
    slots = [{0: shard[0]} for shard in shards]
    for level in range(len(orders[0])):
        for which, order in enumerate(orders):
            step = order[level]
            offsets = sorted(slots[which])
            got = lax.ppermute(
                tuple(slots[which][offset] for offset in offsets),
                axis,
                [(j, j ^ step) for j in range(size)],
            )
            for offset, block in zip(offsets, got):
                slots[which][offset ^ step] = block
    return [
        jnp.concatenate([held[offset] for offset in range(size)], axis=0) for held in slots
    ]


def butterfly_sum(value, axis, size):
    if size & (size - 1):
        return lax.psum(value, axis)
    step = 1
    while step < size:
        value = value + lax.ppermute(value, axis, [(j, j ^ step) for j in range(size)])
        step *= 2
    return value


@jax.custom_vjp
def xor_blocks(matrix, index):
    count = index.shape[0]
    blocks = matrix.reshape(matrix.shape[0], count, matrix.shape[1] // count)
    return jnp.take(blocks, index, axis=1).reshape(matrix.shape)


def xor_blocks_fwd(matrix, index):
    return xor_blocks(matrix, index), index


def xor_blocks_bwd(index, grad):
    return xor_blocks(grad, index), None


xor_blocks.defvjp(xor_blocks_fwd, xor_blocks_bwd)


def rms_scale(inputs, gain_vector):
    return (
        inputs
        * lax.rsqrt(jnp.mean(inputs * inputs, axis=-1, keepdims=True) + EPSILON)
        * gain_vector
    )


def attend_layer(
    section_input, source, key_mask, query_weight, output_weight, gain_vector, block_index
):
    series_count, seq_length, model_width = section_input.shape
    half_width = model_width // 2
    head_dim = half_width // HEADS
    head_shape = (series_count, seq_length, HEADS, head_dim)
    input_wide = section_input.astype(jnp.float32)
    normed = rms_scale(input_wide, gain_vector)
    normed_source = rms_scale(source.astype(jnp.float32), gain_vector)
    normed_rows = normed.astype(jnp.bfloat16).reshape(series_count * seq_length, model_width)
    if block_index is not None:
        normed_rows = xor_blocks(normed_rows, block_index)
    query_flat = jnp.dot(normed_rows, query_weight, preferred_element_type=jnp.float32)
    queries = query_flat.astype(jnp.bfloat16).reshape(head_shape)
    key_rows = normed_source[..., :half_width].astype(jnp.bfloat16).reshape(head_shape)
    value_rows = normed_source[..., half_width:].astype(jnp.bfloat16).reshape(head_shape)
    scores = jnp.einsum(
        "bqhd,bkhd->bhqk", queries, key_rows, preferred_element_type=jnp.float32
    ) / math.sqrt(head_dim)
    raised = jnp.exp(scores) * key_mask.astype(jnp.float32)[:, None, None, :]
    probs = (raised / jnp.sum(raised, axis=-1, keepdims=True)).astype(jnp.bfloat16)
    mixed = jnp.einsum("bhqk,bkhd->bqhd", probs, value_rows, preferred_element_type=jnp.float32)
    mixed = mixed.astype(jnp.bfloat16).reshape(series_count * seq_length, half_width)
    if block_index is not None:
        mixed = xor_blocks(mixed, block_index)
    update = jnp.dot(mixed, output_weight, preferred_element_type=jnp.float32)
    return (input_wide + update.reshape(series_count, seq_length, model_width)).astype(jnp.bfloat16)


def on_device(history, keymask, codes, plan_table, query_weights, output_weights, gains, cotangent):
    section_index = lax.axis_index("section")
    section_count = lax.axis_size("section")
    half_sections = section_count // 2
    micro_count, series_count, seq_length, model_width = history.shape
    rows = micro_count * series_count
    act_shape = (rows, seq_length, model_width)
    fsdp_count = lax.axis_size("fsdp")
    if fsdp_count & (fsdp_count - 1):
        block_index = None
        query_weight = lax.all_gather(query_weights, "fsdp", axis=1, tiled=True)[0]
        output_weight = lax.all_gather(output_weights, "fsdp", axis=1, tiled=True)[0]
    else:
        block_index = jnp.arange(fsdp_count, dtype=jnp.int32) ^ lax.axis_index("fsdp")
        query_weight, output_weight = butterfly_gathers(
            [query_weights, output_weights], exchange_orders(fsdp_count), "fsdp", fsdp_count
        )
    gain_vector = gains[0]
    code_rows = codes.reshape(micro_count, series_count, seq_length)
    code_count = plan_table.shape[0]
    one_hot = (code_rows[..., None] == jnp.arange(code_count, dtype=jnp.int32)).astype(jnp.bfloat16)
    plan_tokens = jnp.einsum(
        "msln,nd->msld", one_hot, plan_table, preferred_element_type=jnp.float32
    ).astype(jnp.bfloat16).reshape(act_shape)
    key_mask = keymask.reshape(rows, seq_length)
    history_rows = history.reshape(act_shape)

    def encoder_map(layer_input, layer_gain):
        return attend_layer(
            layer_input, layer_input, key_mask, query_weight, output_weight, layer_gain,
            block_index,
        )

    def decoder_map(layer_input, layer_memory, layer_gain):
        return attend_layer(
            layer_input, layer_memory, key_mask, query_weight, output_weight, layer_gain,
            block_index,
        )

    pullbacks = {}
    got_input = None
    got_memory = None
    for tick in range(section_count - 1):
        if tick == 0:
            layer_input = history_rows
        elif tick == half_sections:
            layer_input = plan_tokens
        else:
            layer_input = got_input
        if tick < half_sections:
            output, pull = jax.vjp(encoder_map, layer_input, gain_vector)
            pullbacks[tick] = pull
            if tick == half_sections - 1:
                got_memory = send_to(output, "section", tick, tick + 1)
            else:
                got_input = send_to(output, "section", tick, tick + 1)
        else:
            output, pull = jax.vjp(decoder_map, layer_input, got_memory, gain_vector)
            pullbacks[tick] = pull
            got_input, got_memory = send_to((output, got_memory), "section", tick, tick + 1)
    last = section_count - 1
    if last == half_sections:
        last_input = plan_tokens
    else:
        last_input = got_input
    pullbacks[last] = jax.vjp(decoder_map, last_input, got_memory, gain_vector)[1]

    zero_gain = jnp.zeros_like(gain_vector)
    grads_out = jnp.zeros(act_shape, jnp.bfloat16)
    gain_total = zero_gain
    got_grad = None
    got_memory_grad = None
    for tick in range(section_count):
        run = section_count - 1 - tick
        out_grad = cotangent.reshape(act_shape) if run == section_count - 1 else got_grad
        pull = pullbacks[run]
        mine = section_index == run
        if run >= half_sections:
            input_grad, memory_grad, gain_grad = pull(out_grad)
            if got_memory_grad is not None:
                memory_grad = got_memory_grad + memory_grad
            if run == half_sections:
                got_grad = send_to(memory_grad, "section", run, run - 1)
            else:
                got_grad, got_memory_grad = send_to(
                    (input_grad, memory_grad), "section", run, run - 1
                )
        else:
            input_grad, gain_grad = pull(out_grad)
            if run > 0:
                got_grad = send_to(input_grad, "section", run, run - 1)
        grads_out = jnp.where(mine, input_grad, grads_out)
        gain_total = gain_total + jnp.where(mine, gain_grad, zero_gain)
    gain_total = butterfly_sum(gain_total, "fsdp", fsdp_count)
    grads_out = grads_out.reshape(history.shape)
    return (grads_out[None], gain_total[None])


def solution(mesh):
    return jax.shard_map(
        on_device,
        mesh=mesh,
        in_specs=(
            P(None, "fsdp", None, None),
            P(None, "fsdp", None),
            P(None, "fsdp", None, None),
            P(),
            P("section", "fsdp", None),
            P("section", "fsdp", None),
            P("section", None),
            P(None, "fsdp", None, None),
        ),
        out_specs=(P("section", None, "fsdp", None, None), P("section", None)),
        check_vma=False,
    )
```

```python
import math

import jax
import jax.numpy as jnp
from jax import lax
from jax.sharding import PartitionSpec as P

HEADS = 8


EPSILON = 1e-05


def send_to(arrays, axis, source, target):
    return lax.ppermute(arrays, axis, [(source, target)])


def exchange_orders(size):
    steps = []
    step = size // 2
    while step >= 1:
        steps.append(step)
        step //= 2
    other = list(steps)
    if len(other) >= 3:
        other[1], other[2] = other[2], other[1]
    return steps, other


def butterfly_gathers(shards, orders, axis, size):
    index = lax.axis_index(axis)
    held = [shard for shard in shards]
    for level in range(len(orders[0])):
        for which, order in enumerate(orders):
            step = order[level]
            other = lax.ppermute(held[which], axis, [(j, j ^ step) for j in range(size)])
            upper = ((index // step) % 2) == 1
            low = jnp.where(upper, other, held[which])
            high = jnp.where(upper, held[which], other)
            held[which] = jnp.stack([low, high], axis=1).reshape(
                (-1,) + held[which].shape[1:]
            )
    results = []
    for which, order in enumerate(orders):
        block_rows, width = held[which].shape[1:]
        wanted = sorted(order, reverse=True)
        if order != wanted:
            split = held[which].reshape(tuple(2 for _ in order) + (block_rows, width))
            axes = tuple(order.index(value) for value in wanted) + (len(order), len(order) + 1)
            held[which] = jnp.transpose(split, axes)
        results.append(held[which].reshape(size * block_rows, width))
    return results


def butterfly_sum(value, axis, size):
    if size & (size - 1):
        return lax.psum(value, axis)
    step = 1
    while step < size:
        value = value + lax.ppermute(value, axis, [(j, j ^ step) for j in range(size)])
        step *= 2
    return value


def rms_scale(inputs, gain_vector):
    return (
        inputs
        * lax.rsqrt(jnp.mean(inputs * inputs, axis=-1, keepdims=True) + EPSILON)
        * gain_vector
    )


def attend_layer(section_input, source, key_mask, query_weight, output_weight, gain_vector):
    series_count, seq_length, model_width = section_input.shape
    half_width = model_width // 2
    head_dim = half_width // HEADS
    head_shape = (series_count, seq_length, HEADS, head_dim)
    input_wide = section_input.astype(jnp.float32)
    normed = rms_scale(input_wide, gain_vector)
    normed_source = rms_scale(source.astype(jnp.float32), gain_vector)
    normed_rows = normed.astype(jnp.bfloat16).reshape(series_count * seq_length, model_width)
    query_flat = jnp.dot(normed_rows, query_weight, preferred_element_type=jnp.float32)
    queries = query_flat.astype(jnp.bfloat16).reshape(head_shape)
    key_rows = normed_source[..., :half_width].astype(jnp.bfloat16).reshape(head_shape)
    value_rows = normed_source[..., half_width:].astype(jnp.bfloat16).reshape(head_shape)
    scores = jnp.einsum(
        "bqhd,bkhd->bhqk", queries, key_rows, preferred_element_type=jnp.float32
    ) / math.sqrt(head_dim)
    raised = jnp.exp(scores) * key_mask.astype(jnp.float32)[:, None, None, :]
    probs = (raised / jnp.sum(raised, axis=-1, keepdims=True)).astype(jnp.bfloat16)
    mixed = jnp.einsum("bhqk,bkhd->bqhd", probs, value_rows, preferred_element_type=jnp.float32)
    mixed = mixed.astype(jnp.bfloat16).reshape(series_count * seq_length, half_width)
    update = jnp.dot(mixed, output_weight, preferred_element_type=jnp.float32)
    return (input_wide + update.reshape(series_count, seq_length, model_width)).astype(jnp.bfloat16)


def two_section_relay(
    history_rows, plan_tokens, cotangent_rows, key_mask, query_weight, output_weight, gain_vector
):
    is_encoder = lax.axis_index("section") == 0
    half = history_rows.shape[0] // 2

    def part(array, which):
        return array[which * half:(which + 1) * half]

    def pick(encoder_value, decoder_value):
        return jnp.where(is_encoder, encoder_value, decoder_value)

    def layer_vjp(layer_input, layer_source, layer_mask, out_grad):
        def apply(x, source, layer_gain):
            return attend_layer(x, source, layer_mask, query_weight, output_weight, layer_gain)

        output, pull = jax.vjp(apply, layer_input, layer_source, gain_vector)
        return (output,) + pull(out_grad)

    both_ways = [(0, 1), (1, 0)]
    zero_gain = jnp.zeros_like(gain_vector)
    hist_a, hist_b = part(history_rows, 0), part(history_rows, 1)
    mask_a, mask_b = part(key_mask, 0), part(key_mask, 1)
    plan_a, plan_b = part(plan_tokens, 0), part(plan_tokens, 1)
    memory_a = attend_layer(hist_a, hist_a, mask_a, query_weight, output_weight, gain_vector)
    memory_a = send_to(memory_a, "section", 0, 1)
    memory_b, input_grad, memory_grad, gain_1 = layer_vjp(
        pick(hist_b, plan_a),
        pick(hist_b, memory_a),
        pick(mask_b, mask_a),
        pick(jnp.zeros_like(hist_b), part(cotangent_rows, 0)),
    )
    decoder_grad_a = input_grad
    received = lax.ppermute(pick(memory_b, memory_grad), "section", both_ways)
    _, input_grad, memory_grad, gain_2 = layer_vjp(
        pick(hist_a, plan_b),
        pick(hist_a, received),
        pick(mask_a, mask_b),
        pick(received, part(cotangent_rows, 1)),
    )
    encoder_grad_a = input_grad + memory_grad
    decoder_grad_b = input_grad
    memory_grad_b = send_to(memory_grad, "section", 1, 0)
    _, input_grad, memory_grad, gain_3 = layer_vjp(hist_b, hist_b, mask_b, memory_grad_b)
    encoder_grad_b = input_grad + memory_grad
    grads = jnp.concatenate(
        [pick(encoder_grad_a, decoder_grad_a), pick(encoder_grad_b, decoder_grad_b)], axis=0
    )
    gain_total = pick(zero_gain, gain_1) + gain_2 + pick(gain_3, zero_gain)
    return grads, gain_total


def on_device(history, keymask, codes, plan_table, query_weights, output_weights, gains, cotangent):
    section_index = lax.axis_index("section")
    section_count = lax.axis_size("section")
    half_sections = section_count // 2
    micro_count, series_count, seq_length, model_width = history.shape
    rows = micro_count * series_count
    act_shape = (rows, seq_length, model_width)
    fsdp_count = lax.axis_size("fsdp")
    if fsdp_count & (fsdp_count - 1):
        query_weight = lax.all_gather(query_weights, "fsdp", axis=1, tiled=True)[0]
        output_weight = lax.all_gather(output_weights, "fsdp", axis=1, tiled=True)[0]
    else:
        query_weight, output_weight = butterfly_gathers(
            [query_weights, output_weights], exchange_orders(fsdp_count), "fsdp", fsdp_count
        )
    gain_vector = gains[0]
    code_rows = codes.reshape(micro_count, series_count, seq_length)
    code_count = plan_table.shape[0]
    one_hot = (code_rows[..., None] == jnp.arange(code_count, dtype=jnp.int32)).astype(jnp.bfloat16)
    plan_tokens = jnp.einsum(
        "msln,nd->msld", one_hot, plan_table, preferred_element_type=jnp.float32
    ).astype(jnp.bfloat16).reshape(act_shape)
    key_mask = keymask.reshape(rows, seq_length)
    history_rows = history.reshape(act_shape)
    if section_count == 2 and micro_count % 2 == 0:
        grads_out, gain_total = two_section_relay(
            history_rows, plan_tokens, cotangent.reshape(act_shape), key_mask,
            query_weight, output_weight, gain_vector,
        )
        gain_total = butterfly_sum(gain_total, "fsdp", fsdp_count)
        return (grads_out.reshape(history.shape)[None], gain_total[None])

    def encoder_map(layer_input, layer_gain):
        return attend_layer(
            layer_input, layer_input, key_mask, query_weight, output_weight, layer_gain
        )

    def decoder_map(layer_input, layer_memory, layer_gain):
        return attend_layer(
            layer_input, layer_memory, key_mask, query_weight, output_weight, layer_gain
        )

    saved_inputs = {}
    got_input = None
    got_memory = None
    for tick in range(section_count - 1):
        if tick == 0:
            layer_input = history_rows
        elif tick == half_sections:
            layer_input = plan_tokens
        else:
            layer_input = got_input
        if tick < half_sections:
            output = encoder_map(layer_input, gain_vector)
            saved_inputs[tick] = (layer_input, None)
            if tick == half_sections - 1:
                got_memory = send_to(output, "section", tick, tick + 1)
            else:
                got_input = send_to(output, "section", tick, tick + 1)
        else:
            output = decoder_map(layer_input, got_memory, gain_vector)
            saved_inputs[tick] = (layer_input, got_memory)
            got_input, got_memory = send_to((output, got_memory), "section", tick, tick + 1)
    last = section_count - 1
    if last == half_sections:
        saved_inputs[last] = (plan_tokens, got_memory)
    else:
        saved_inputs[last] = (got_input, got_memory)

    zero_gain = jnp.zeros_like(gain_vector)
    grads_out = jnp.zeros(act_shape, jnp.bfloat16)
    gain_total = zero_gain
    got_grad = None
    got_memory_grad = None
    for tick in range(section_count):
        run = section_count - 1 - tick
        out_grad = cotangent.reshape(act_shape) if run == section_count - 1 else got_grad
        layer_input, layer_memory = saved_inputs[run]
        mine = section_index == run
        if run >= half_sections:
            _, pull = jax.vjp(decoder_map, layer_input, layer_memory, gain_vector)
            input_grad, memory_grad, gain_grad = pull(out_grad)
            if got_memory_grad is not None:
                memory_grad = got_memory_grad + memory_grad
            if run == half_sections:
                got_grad = send_to(memory_grad, "section", run, run - 1)
            else:
                got_grad, got_memory_grad = send_to(
                    (input_grad, memory_grad), "section", run, run - 1
                )
        else:
            _, pull = jax.vjp(encoder_map, layer_input, gain_vector)
            input_grad, gain_grad = pull(out_grad)
            if run > 0:
                got_grad = send_to(input_grad, "section", run, run - 1)
        grads_out = jnp.where(mine, input_grad, grads_out)
        gain_total = gain_total + jnp.where(mine, gain_grad, zero_gain)
    gain_total = butterfly_sum(gain_total, "fsdp", fsdp_count)
    grads_out = grads_out.reshape(history.shape)
    return (grads_out[None], gain_total[None])


def solution(mesh):
    return jax.shard_map(
        on_device,
        mesh=mesh,
        in_specs=(
            P(None, "fsdp", None, None),
            P(None, "fsdp", None),
            P(None, "fsdp", None, None),
            P(),
            P("section", "fsdp", None),
            P("section", "fsdp", None),
            P("section", None),
            P(None, "fsdp", None, None),
        ),
        out_specs=(P("section", None, "fsdp", None, None), P("section", None)),
        check_vma=False,
    )
```

```python
import math

import jax
import jax.numpy as jnp
from jax import lax
from jax.sharding import PartitionSpec as P

HEADS = 8


EPSILON = 1e-05


def send_to(arrays, axis, source, target):
    return lax.ppermute(arrays, axis, [(source, target)])


def exchange_orders(size):
    steps = []
    step = size // 2
    while step >= 1:
        steps.append(step)
        step //= 2
    other = list(steps)
    if len(other) >= 3:
        other[1], other[2] = other[2], other[1]
    return steps, other


def butterfly_gathers(shards, orders, axis, size):
    index = lax.axis_index(axis)
    held = [shard[0][None] for shard in shards]
    done = [[] for _ in shards]
    for level in range(len(orders[0]) - 1):
        for which, order in enumerate(orders):
            step = order[level]
            other = lax.ppermute(held[which], axis, [(j, j ^ step) for j in range(size)])
            upper = ((index // step) % 2) == 1
            low = jnp.where(upper, other, held[which])
            high = jnp.where(upper, held[which], other)
            grid = (2,) * len(done[which]) + held[which].shape[1:]
            place = sum(1 for value in done[which] if value > step)
            held[which] = jnp.stack(
                [low.reshape(grid), high.reshape(grid)], axis=place
            ).reshape((-1,) + held[which].shape[1:])
            done[which].append(step)
    pairs = []
    for which, order in enumerate(orders):
        other = lax.ppermute(held[which], axis, [(j, j ^ order[-1]) for j in range(size)])
        block_rows, width = held[which].shape[1:]
        pairs.append((held[which].reshape(-1, width), other.reshape(-1, width), block_rows))
    return pairs


def split_product(rows, pair, own_bit):
    mine, theirs, block_rows = pair
    grid = rows.reshape(rows.shape[0], -1, 2, block_rows)
    own_part = lax.dynamic_index_in_dim(grid, own_bit, 2, False).reshape(rows.shape[0], -1)
    other_part = lax.dynamic_index_in_dim(grid, 1 - own_bit, 2, False).reshape(rows.shape[0], -1)
    return jnp.dot(own_part, mine, preferred_element_type=jnp.float32) + jnp.dot(
        other_part, theirs, preferred_element_type=jnp.float32
    )


def butterfly_sum(value, axis, size):
    if size & (size - 1):
        return lax.psum(value, axis)
    step = 1
    while step < size:
        value = value + lax.ppermute(value, axis, [(j, j ^ step) for j in range(size)])
        step *= 2
    return value


def rms_scale(inputs, gain_vector):
    return (
        inputs
        * lax.rsqrt(jnp.mean(inputs * inputs, axis=-1, keepdims=True) + EPSILON)
        * gain_vector
    )


def attend_layer(section_input, source, key_mask, project_query, project_output, gain_vector):
    series_count, seq_length, model_width = section_input.shape
    half_width = model_width // 2
    head_dim = half_width // HEADS
    head_shape = (series_count, seq_length, HEADS, head_dim)
    input_wide = section_input.astype(jnp.float32)
    normed = rms_scale(input_wide, gain_vector)
    normed_source = rms_scale(source.astype(jnp.float32), gain_vector)
    normed_rows = normed.astype(jnp.bfloat16).reshape(series_count * seq_length, model_width)
    query_flat = project_query(normed_rows)
    queries = query_flat.astype(jnp.bfloat16).reshape(head_shape)
    key_rows = normed_source[..., :half_width].astype(jnp.bfloat16).reshape(head_shape)
    value_rows = normed_source[..., half_width:].astype(jnp.bfloat16).reshape(head_shape)
    scores = jnp.einsum(
        "bqhd,bkhd->bhqk", queries, key_rows, preferred_element_type=jnp.float32
    ) / math.sqrt(head_dim)
    raised = jnp.exp(scores) * key_mask.astype(jnp.float32)[:, None, None, :]
    probs = (raised / jnp.sum(raised, axis=-1, keepdims=True)).astype(jnp.bfloat16)
    mixed = jnp.einsum("bhqk,bkhd->bqhd", probs, value_rows, preferred_element_type=jnp.float32)
    mixed = mixed.astype(jnp.bfloat16).reshape(series_count * seq_length, half_width)
    update = project_output(mixed)
    return (input_wide + update.reshape(series_count, seq_length, model_width)).astype(jnp.bfloat16)


def on_device(history, keymask, codes, plan_table, query_weights, output_weights, gains, cotangent):
    section_index = lax.axis_index("section")
    section_count = lax.axis_size("section")
    half_sections = section_count // 2
    micro_count, series_count, seq_length, model_width = history.shape
    rows = micro_count * series_count
    act_shape = (rows, seq_length, model_width)
    fsdp_count = lax.axis_size("fsdp")
    if fsdp_count < 2 or fsdp_count & (fsdp_count - 1):
        query_weight = lax.all_gather(query_weights, "fsdp", axis=1, tiled=True)[0]
        output_weight = lax.all_gather(output_weights, "fsdp", axis=1, tiled=True)[0]

        def query_weight(rows, weight=query_weight):
            return jnp.dot(rows, weight, preferred_element_type=jnp.float32)

        def output_weight(rows, weight=output_weight):
            return jnp.dot(rows, weight, preferred_element_type=jnp.float32)
    else:
        own_bit = lax.axis_index("fsdp") % 2
        query_pair, output_pair = butterfly_gathers(
            [query_weights, output_weights], exchange_orders(fsdp_count), "fsdp", fsdp_count
        )

        def query_weight(rows):
            return split_product(rows, query_pair, own_bit)

        def output_weight(rows):
            return split_product(rows, output_pair, own_bit)
    gain_vector = gains[0]
    code_rows = codes.reshape(micro_count, series_count, seq_length)
    code_count = plan_table.shape[0]
    one_hot = (code_rows[..., None] == jnp.arange(code_count, dtype=jnp.int32)).astype(jnp.bfloat16)
    plan_tokens = jnp.einsum(
        "msln,nd->msld", one_hot, plan_table, preferred_element_type=jnp.float32
    ).astype(jnp.bfloat16).reshape(act_shape)
    key_mask = keymask.reshape(rows, seq_length)
    history_rows = history.reshape(act_shape)

    def encoder_map(layer_input, layer_gain):
        return attend_layer(
            layer_input, layer_input, key_mask, query_weight, output_weight, layer_gain
        )

    def decoder_map(layer_input, layer_memory, layer_gain):
        return attend_layer(
            layer_input, layer_memory, key_mask, query_weight, output_weight, layer_gain
        )

    saved_inputs = {}
    got_input = None
    got_memory = None
    for tick in range(section_count - 1):
        if tick == 0:
            layer_input = history_rows
        elif tick == half_sections:
            layer_input = plan_tokens
        else:
            layer_input = got_input
        if tick < half_sections:
            output = encoder_map(layer_input, gain_vector)
            saved_inputs[tick] = (layer_input, None)
            if tick == half_sections - 1:
                got_memory = send_to(output, "section", tick, tick + 1)
            else:
                got_input = send_to(output, "section", tick, tick + 1)
        else:
            output = decoder_map(layer_input, got_memory, gain_vector)
            saved_inputs[tick] = (layer_input, got_memory)
            got_input, got_memory = send_to((output, got_memory), "section", tick, tick + 1)
    last = section_count - 1
    if last == half_sections:
        saved_inputs[last] = (plan_tokens, got_memory)
    else:
        saved_inputs[last] = (got_input, got_memory)

    zero_gain = jnp.zeros_like(gain_vector)
    grads_out = jnp.zeros(act_shape, jnp.bfloat16)
    gain_total = zero_gain
    got_grad = None
    got_memory_grad = None
    for tick in range(section_count):
        run = section_count - 1 - tick
        out_grad = cotangent.reshape(act_shape) if run == section_count - 1 else got_grad
        layer_input, layer_memory = saved_inputs[run]
        mine = section_index == run
        if run >= half_sections:
            _, pull = jax.vjp(decoder_map, layer_input, layer_memory, gain_vector)
            input_grad, memory_grad, gain_grad = pull(out_grad)
            if got_memory_grad is not None:
                memory_grad = got_memory_grad + memory_grad
            if run == half_sections:
                got_grad = send_to(memory_grad, "section", run, run - 1)
            else:
                got_grad, got_memory_grad = send_to(
                    (input_grad, memory_grad), "section", run, run - 1
                )
        else:
            _, pull = jax.vjp(encoder_map, layer_input, gain_vector)
            input_grad, gain_grad = pull(out_grad)
            if run > 0:
                got_grad = send_to(input_grad, "section", run, run - 1)
        grads_out = jnp.where(mine, input_grad, grads_out)
        gain_total = gain_total + jnp.where(mine, gain_grad, zero_gain)
    gain_total = butterfly_sum(gain_total, "fsdp", fsdp_count)
    grads_out = grads_out.reshape(history.shape)
    return (grads_out[None], gain_total[None])


def solution(mesh):
    return jax.shard_map(
        on_device,
        mesh=mesh,
        in_specs=(
            P(None, "fsdp", None, None),
            P(None, "fsdp", None),
            P(None, "fsdp", None, None),
            P(),
            P("section", "fsdp", None),
            P("section", "fsdp", None),
            P("section", None),
            P(None, "fsdp", None, None),
        ),
        out_specs=(P("section", None, "fsdp", None, None), P("section", None)),
        check_vma=False,
    )
```

```python
import math

import jax
import jax.numpy as jnp
from jax import lax
from jax.sharding import PartitionSpec as P

HEADS = 8


EPSILON = 1e-05


def send_to(arrays, axis, source, target):
    return lax.ppermute(arrays, axis, [(source, target)])


def exchange_orders(size):
    steps = []
    step = size // 2
    while step >= 1:
        steps.append(step)
        step //= 2
    other = list(steps)
    if len(other) >= 3:
        other[1], other[2] = other[2], other[1]
    return steps, other


def butterfly_gathers(shards, orders, axis, size):
    index = lax.axis_index(axis)
    held = [shard[0][None] for shard in shards]
    done = [[] for _ in shards]
    for level in range(len(orders[0]) - 1):
        for which, order in enumerate(orders):
            step = order[level]
            other = lax.ppermute(held[which], axis, [(j, j ^ step) for j in range(size)])
            upper = ((index // step) % 2) == 1
            low = jnp.where(upper, other, held[which])
            high = jnp.where(upper, held[which], other)
            grid = (2,) * len(done[which]) + held[which].shape[1:]
            place = sum(1 for value in done[which] if value > step)
            held[which] = jnp.stack(
                [low.reshape(grid), high.reshape(grid)], axis=place
            ).reshape((-1,) + held[which].shape[1:])
            done[which].append(step)
    pairs = []
    for which, order in enumerate(orders):
        other = lax.ppermute(held[which], axis, [(j, j ^ order[-1]) for j in range(size)])
        block_rows, width = held[which].shape[1:]
        pairs.append((held[which].reshape(-1, width), other.reshape(-1, width), block_rows))
    return pairs


def split_product(rows, pair, own_bit):
    mine, theirs, block_rows = pair
    grid = rows.reshape(rows.shape[0], -1, 2, block_rows)
    even = grid[:, :, 0].reshape(rows.shape[0], -1)
    odd = grid[:, :, 1].reshape(rows.shape[0], -1)
    own_part = jnp.where(own_bit == 0, even, odd)
    other_part = jnp.where(own_bit == 0, odd, even)
    return jnp.dot(own_part, mine, preferred_element_type=jnp.float32) + jnp.dot(
        other_part, theirs, preferred_element_type=jnp.float32
    )


def butterfly_sum(value, axis, size):
    if size & (size - 1):
        return lax.psum(value, axis)
    step = 1
    while step < size:
        value = value + lax.ppermute(value, axis, [(j, j ^ step) for j in range(size)])
        step *= 2
    return value


def rms_scale(inputs, gain_vector):
    return (
        inputs
        * lax.rsqrt(jnp.mean(inputs * inputs, axis=-1, keepdims=True) + EPSILON)
        * gain_vector
    )


def attend_layer(section_input, source, key_mask, project_query, project_output, gain_vector):
    series_count, seq_length, model_width = section_input.shape
    half_width = model_width // 2
    head_dim = half_width // HEADS
    head_shape = (series_count, seq_length, HEADS, head_dim)
    input_wide = section_input.astype(jnp.float32)
    normed = rms_scale(input_wide, gain_vector)
    normed_source = rms_scale(source.astype(jnp.float32), gain_vector)
    normed_rows = normed.astype(jnp.bfloat16).reshape(series_count * seq_length, model_width)
    query_flat = project_query(normed_rows)
    queries = query_flat.astype(jnp.bfloat16).reshape(head_shape)
    key_rows = normed_source[..., :half_width].astype(jnp.bfloat16).reshape(head_shape)
    value_rows = normed_source[..., half_width:].astype(jnp.bfloat16).reshape(head_shape)
    scores = jnp.einsum(
        "bqhd,bkhd->bhqk", queries, key_rows, preferred_element_type=jnp.float32
    ) / math.sqrt(head_dim)
    raised = jnp.exp(scores) * key_mask.astype(jnp.float32)[:, None, None, :]
    probs = (raised / jnp.sum(raised, axis=-1, keepdims=True)).astype(jnp.bfloat16)
    mixed = jnp.einsum("bhqk,bkhd->bqhd", probs, value_rows, preferred_element_type=jnp.float32)
    mixed = mixed.astype(jnp.bfloat16).reshape(series_count * seq_length, half_width)
    update = project_output(mixed)
    return (input_wide + update.reshape(series_count, seq_length, model_width)).astype(jnp.bfloat16)


def on_device(history, keymask, codes, plan_table, query_weights, output_weights, gains, cotangent):
    section_index = lax.axis_index("section")
    section_count = lax.axis_size("section")
    half_sections = section_count // 2
    micro_count, series_count, seq_length, model_width = history.shape
    rows = micro_count * series_count
    act_shape = (rows, seq_length, model_width)
    fsdp_count = lax.axis_size("fsdp")
    if fsdp_count < 2 or fsdp_count & (fsdp_count - 1):
        query_weight = lax.all_gather(query_weights, "fsdp", axis=1, tiled=True)[0]
        output_weight = lax.all_gather(output_weights, "fsdp", axis=1, tiled=True)[0]

        def query_weight(rows, weight=query_weight):
            return jnp.dot(rows, weight, preferred_element_type=jnp.float32)

        def output_weight(rows, weight=output_weight):
            return jnp.dot(rows, weight, preferred_element_type=jnp.float32)
    else:
        own_bit = lax.axis_index("fsdp") % 2
        query_pair, output_pair = butterfly_gathers(
            [query_weights, output_weights], exchange_orders(fsdp_count), "fsdp", fsdp_count
        )

        def query_weight(rows):
            return split_product(rows, query_pair, own_bit)

        def output_weight(rows):
            return split_product(rows, output_pair, own_bit)
    gain_vector = gains[0]
    code_rows = codes.reshape(micro_count, series_count, seq_length)
    code_count = plan_table.shape[0]
    one_hot = (code_rows[..., None] == jnp.arange(code_count, dtype=jnp.int32)).astype(jnp.bfloat16)
    plan_tokens = jnp.einsum(
        "msln,nd->msld", one_hot, plan_table, preferred_element_type=jnp.float32
    ).astype(jnp.bfloat16).reshape(act_shape)
    key_mask = keymask.reshape(rows, seq_length)
    history_rows = history.reshape(act_shape)

    def encoder_map(layer_input, layer_gain):
        return attend_layer(
            layer_input, layer_input, key_mask, query_weight, output_weight, layer_gain
        )

    def decoder_map(layer_input, layer_memory, layer_gain):
        return attend_layer(
            layer_input, layer_memory, key_mask, query_weight, output_weight, layer_gain
        )

    saved_inputs = {}
    got_input = None
    got_memory = None
    for tick in range(section_count - 1):
        if tick == 0:
            layer_input = history_rows
        elif tick == half_sections:
            layer_input = plan_tokens
        else:
            layer_input = got_input
        if tick < half_sections:
            output = encoder_map(layer_input, gain_vector)
            saved_inputs[tick] = (layer_input, None)
            if tick == half_sections - 1:
                got_memory = send_to(output, "section", tick, tick + 1)
            else:
                got_input = send_to(output, "section", tick, tick + 1)
        else:
            output = decoder_map(layer_input, got_memory, gain_vector)
            saved_inputs[tick] = (layer_input, got_memory)
            got_input, got_memory = send_to((output, got_memory), "section", tick, tick + 1)
    last = section_count - 1
    if last == half_sections:
        saved_inputs[last] = (plan_tokens, got_memory)
    else:
        saved_inputs[last] = (got_input, got_memory)

    zero_gain = jnp.zeros_like(gain_vector)
    grads_out = jnp.zeros(act_shape, jnp.bfloat16)
    gain_total = zero_gain
    got_grad = None
    got_memory_grad = None
    for tick in range(section_count):
        run = section_count - 1 - tick
        out_grad = cotangent.reshape(act_shape) if run == section_count - 1 else got_grad
        layer_input, layer_memory = saved_inputs[run]
        mine = section_index == run
        if run >= half_sections:
            _, pull = jax.vjp(decoder_map, layer_input, layer_memory, gain_vector)
            input_grad, memory_grad, gain_grad = pull(out_grad)
            if got_memory_grad is not None:
                memory_grad = got_memory_grad + memory_grad
            if run == half_sections:
                got_grad = send_to(memory_grad, "section", run, run - 1)
            else:
                got_grad, got_memory_grad = send_to(
                    (input_grad, memory_grad), "section", run, run - 1
                )
        else:
            _, pull = jax.vjp(encoder_map, layer_input, gain_vector)
            input_grad, gain_grad = pull(out_grad)
            if run > 0:
                got_grad = send_to(input_grad, "section", run, run - 1)
        grads_out = jnp.where(mine, input_grad, grads_out)
        gain_total = gain_total + jnp.where(mine, gain_grad, zero_gain)
    gain_total = butterfly_sum(gain_total, "fsdp", fsdp_count)
    grads_out = grads_out.reshape(history.shape)
    return (grads_out[None], gain_total[None])


def solution(mesh):
    return jax.shard_map(
        on_device,
        mesh=mesh,
        in_specs=(
            P(None, "fsdp", None, None),
            P(None, "fsdp", None),
            P(None, "fsdp", None, None),
            P(),
            P("section", "fsdp", None),
            P("section", "fsdp", None),
            P("section", None),
            P(None, "fsdp", None, None),
        ),
        out_specs=(P("section", None, "fsdp", None, None), P("section", None)),
        check_vma=False,
    )
```

```python
import math

import jax
import jax.numpy as jnp
from jax import lax
from jax.sharding import PartitionSpec as P

HEADS = 8


EPSILON = 1e-05


def send_to(arrays, axis, source, target):
    return lax.ppermute(arrays, axis, [(source, target)])


def exchange_orders(size):
    steps = []
    step = size // 2
    while step >= 1:
        steps.append(step)
        step //= 2
    other = list(steps)
    if len(other) >= 3:
        other[1], other[2] = other[2], other[1]
    return steps, other


def butterfly_gathers(shards, orders, axis, size):
    index = lax.axis_index(axis)
    held = [shard[0][None] for shard in shards]
    done = [[] for _ in shards]
    for level in range(len(orders[0]) - 1):
        for which, order in enumerate(orders):
            step = order[level]
            other = lax.ppermute(held[which], axis, [(j, j ^ step) for j in range(size)])
            upper = ((index // step) % 2) == 1
            low = jnp.where(upper, other, held[which])
            high = jnp.where(upper, held[which], other)
            grid = (2,) * len(done[which]) + held[which].shape[1:]
            place = sum(1 for value in done[which] if value > step)
            held[which] = jnp.stack(
                [low.reshape(grid), high.reshape(grid)], axis=place
            ).reshape((-1,) + held[which].shape[1:])
            done[which].append(step)
    pairs = []
    for which, order in enumerate(orders):
        other = lax.ppermute(held[which], axis, [(j, j ^ order[-1]) for j in range(size)])
        block_rows, width = held[which].shape[1:]
        pairs.append((held[which].reshape(-1, width), other.reshape(-1, width), block_rows))
    return pairs


def split_product(rows, pair, own_bit):
    mine, theirs, block_rows = pair
    grid = rows.reshape(rows.shape[0], -1, 2 * block_rows)
    even = grid[:, :, :block_rows].reshape(rows.shape[0], -1)
    odd = grid[:, :, block_rows:].reshape(rows.shape[0], -1)
    own_part = jnp.where(own_bit == 0, even, odd)
    other_part = jnp.where(own_bit == 0, odd, even)
    return jnp.dot(own_part, mine, preferred_element_type=jnp.float32) + jnp.dot(
        other_part, theirs, preferred_element_type=jnp.float32
    )


def butterfly_sum(value, axis, size):
    if size & (size - 1):
        return lax.psum(value, axis)
    step = 1
    while step < size:
        value = value + lax.ppermute(value, axis, [(j, j ^ step) for j in range(size)])
        step *= 2
    return value


def rms_scale(inputs, gain_vector):
    return (
        inputs
        * lax.rsqrt(jnp.mean(inputs * inputs, axis=-1, keepdims=True) + EPSILON)
        * gain_vector
    )


def attend_layer(section_input, source, key_mask, project_query, project_output, gain_vector):
    series_count, seq_length, model_width = section_input.shape
    half_width = model_width // 2
    head_dim = half_width // HEADS
    head_shape = (series_count, seq_length, HEADS, head_dim)
    input_wide = section_input.astype(jnp.float32)
    normed = rms_scale(input_wide, gain_vector)
    normed_source = rms_scale(source.astype(jnp.float32), gain_vector)
    normed_rows = normed.astype(jnp.bfloat16).reshape(series_count * seq_length, model_width)
    query_flat = project_query(normed_rows)
    queries = query_flat.astype(jnp.bfloat16).reshape(head_shape)
    key_rows = normed_source[..., :half_width].astype(jnp.bfloat16).reshape(head_shape)
    value_rows = normed_source[..., half_width:].astype(jnp.bfloat16).reshape(head_shape)
    scores = jnp.einsum(
        "bqhd,bkhd->bhqk", queries, key_rows, preferred_element_type=jnp.float32
    ) / math.sqrt(head_dim)
    raised = jnp.exp(scores) * key_mask.astype(jnp.float32)[:, None, None, :]
    probs = (raised / jnp.sum(raised, axis=-1, keepdims=True)).astype(jnp.bfloat16)
    mixed = jnp.einsum("bhqk,bkhd->bqhd", probs, value_rows, preferred_element_type=jnp.float32)
    mixed = mixed.astype(jnp.bfloat16).reshape(series_count * seq_length, half_width)
    update = project_output(mixed)
    return (input_wide + update.reshape(series_count, seq_length, model_width)).astype(jnp.bfloat16)


def on_device(history, keymask, codes, plan_table, query_weights, output_weights, gains, cotangent):
    section_index = lax.axis_index("section")
    section_count = lax.axis_size("section")
    half_sections = section_count // 2
    micro_count, series_count, seq_length, model_width = history.shape
    rows = micro_count * series_count
    act_shape = (rows, seq_length, model_width)
    fsdp_count = lax.axis_size("fsdp")
    if fsdp_count < 2 or fsdp_count & (fsdp_count - 1):
        query_weight = lax.all_gather(query_weights, "fsdp", axis=1, tiled=True)[0]
        output_weight = lax.all_gather(output_weights, "fsdp", axis=1, tiled=True)[0]

        def query_weight(rows, weight=query_weight):
            return jnp.dot(rows, weight, preferred_element_type=jnp.float32)

        def output_weight(rows, weight=output_weight):
            return jnp.dot(rows, weight, preferred_element_type=jnp.float32)
    else:
        own_bit = lax.axis_index("fsdp") % 2
        query_pair, output_pair = butterfly_gathers(
            [query_weights, output_weights], exchange_orders(fsdp_count), "fsdp", fsdp_count
        )

        def query_weight(rows):
            return split_product(rows, query_pair, own_bit)

        def output_weight(rows):
            return split_product(rows, output_pair, own_bit)
    gain_vector = gains[0]
    code_rows = codes.reshape(micro_count, series_count, seq_length)
    code_count = plan_table.shape[0]
    one_hot = (code_rows[..., None] == jnp.arange(code_count, dtype=jnp.int32)).astype(jnp.bfloat16)
    plan_tokens = jnp.einsum(
        "msln,nd->msld", one_hot, plan_table, preferred_element_type=jnp.float32
    ).astype(jnp.bfloat16).reshape(act_shape)
    key_mask = keymask.reshape(rows, seq_length)
    history_rows = history.reshape(act_shape)

    def encoder_map(layer_input, layer_gain):
        return attend_layer(
            layer_input, layer_input, key_mask, query_weight, output_weight, layer_gain
        )

    def decoder_map(layer_input, layer_memory, layer_gain):
        return attend_layer(
            layer_input, layer_memory, key_mask, query_weight, output_weight, layer_gain
        )

    saved_inputs = {}
    got_input = None
    got_memory = None
    for tick in range(section_count - 1):
        if tick == 0:
            layer_input = history_rows
        elif tick == half_sections:
            layer_input = plan_tokens
        else:
            layer_input = got_input
        if tick < half_sections:
            output = encoder_map(layer_input, gain_vector)
            saved_inputs[tick] = (layer_input, None)
            if tick == half_sections - 1:
                got_memory = send_to(output, "section", tick, tick + 1)
            else:
                got_input = send_to(output, "section", tick, tick + 1)
        else:
            output = decoder_map(layer_input, got_memory, gain_vector)
            saved_inputs[tick] = (layer_input, got_memory)
            got_input, got_memory = send_to((output, got_memory), "section", tick, tick + 1)
    last = section_count - 1
    if last == half_sections:
        saved_inputs[last] = (plan_tokens, got_memory)
    else:
        saved_inputs[last] = (got_input, got_memory)

    zero_gain = jnp.zeros_like(gain_vector)
    grads_out = jnp.zeros(act_shape, jnp.bfloat16)
    gain_total = zero_gain
    got_grad = None
    got_memory_grad = None
    for tick in range(section_count):
        run = section_count - 1 - tick
        out_grad = cotangent.reshape(act_shape) if run == section_count - 1 else got_grad
        layer_input, layer_memory = saved_inputs[run]
        mine = section_index == run
        if run >= half_sections:
            _, pull = jax.vjp(decoder_map, layer_input, layer_memory, gain_vector)
            input_grad, memory_grad, gain_grad = pull(out_grad)
            if got_memory_grad is not None:
                memory_grad = got_memory_grad + memory_grad
            if run == half_sections:
                got_grad = send_to(memory_grad, "section", run, run - 1)
            else:
                got_grad, got_memory_grad = send_to(
                    (input_grad, memory_grad), "section", run, run - 1
                )
        else:
            _, pull = jax.vjp(encoder_map, layer_input, gain_vector)
            input_grad, gain_grad = pull(out_grad)
            if run > 0:
                got_grad = send_to(input_grad, "section", run, run - 1)
        grads_out = jnp.where(mine, input_grad, grads_out)
        gain_total = gain_total + jnp.where(mine, gain_grad, zero_gain)
    gain_total = butterfly_sum(gain_total, "fsdp", fsdp_count)
    grads_out = grads_out.reshape(history.shape)
    return (grads_out[None], gain_total[None])


def solution(mesh):
    return jax.shard_map(
        on_device,
        mesh=mesh,
        in_specs=(
            P(None, "fsdp", None, None),
            P(None, "fsdp", None),
            P(None, "fsdp", None, None),
            P(),
            P("section", "fsdp", None),
            P("section", "fsdp", None),
            P("section", None),
            P(None, "fsdp", None, None),
        ),
        out_specs=(P("section", None, "fsdp", None, None), P("section", None)),
        check_vma=False,
    )
```

```python
import math

import jax
import jax.numpy as jnp
from jax import lax
from jax.sharding import PartitionSpec as P

HEADS = 8


EPSILON = 1e-05


def send_to(arrays, axis, source, target):
    return lax.ppermute(arrays, axis, [(source, target)])


def exchange_orders(size):
    steps = []
    step = size // 2
    while step >= 1:
        steps.append(step)
        step //= 2
    other = list(steps)
    if len(other) >= 3:
        other[1], other[2] = other[2], other[1]
    return steps, other


def butterfly_gathers(shards, orders, axis, size):
    index = lax.axis_index(axis)
    held = [shard for shard in shards]
    for level in range(len(orders[0])):
        for which, order in enumerate(orders):
            step = order[level]
            other = lax.ppermute(held[which], axis, [(j, j ^ step) for j in range(size)])
            upper = ((index // step) % 2) == 1
            mine = held[which]
            held[which] = lax.cond(
                upper,
                lambda a, b: jnp.stack([b, a], axis=1).reshape((-1,) + a.shape[1:]),
                lambda a, b: jnp.stack([a, b], axis=1).reshape((-1,) + a.shape[1:]),
                mine,
                other,
            )
    results = []
    for which, order in enumerate(orders):
        block_rows, width = held[which].shape[1:]
        wanted = sorted(order, reverse=True)
        if order != wanted:
            split = held[which].reshape(tuple(2 for _ in order) + (block_rows, width))
            axes = tuple(order.index(value) for value in wanted) + (len(order), len(order) + 1)
            held[which] = jnp.transpose(split, axes)
        results.append(held[which].reshape(size * block_rows, width))
    return results


def butterfly_sum(value, axis, size):
    if size & (size - 1):
        return lax.psum(value, axis)
    step = 1
    while step < size:
        value = value + lax.ppermute(value, axis, [(j, j ^ step) for j in range(size)])
        step *= 2
    return value


def rms_scale(inputs, gain_vector):
    return (
        inputs
        * lax.rsqrt(jnp.mean(inputs * inputs, axis=-1, keepdims=True) + EPSILON)
        * gain_vector
    )


def attend_layer(section_input, source, key_mask, query_weight, output_weight, gain_vector):
    series_count, seq_length, model_width = section_input.shape
    half_width = model_width // 2
    head_dim = half_width // HEADS
    head_shape = (series_count, seq_length, HEADS, head_dim)
    input_wide = section_input.astype(jnp.float32)
    normed = rms_scale(input_wide, gain_vector)
    normed_source = rms_scale(source.astype(jnp.float32), gain_vector)
    normed_rows = normed.astype(jnp.bfloat16).reshape(series_count * seq_length, model_width)
    query_flat = jnp.dot(normed_rows, query_weight, preferred_element_type=jnp.float32)
    queries = query_flat.astype(jnp.bfloat16).reshape(head_shape)
    key_rows = normed_source[..., :half_width].astype(jnp.bfloat16).reshape(head_shape)
    value_rows = normed_source[..., half_width:].astype(jnp.bfloat16).reshape(head_shape)
    scores = jnp.einsum(
        "bqhd,bkhd->bhqk", queries, key_rows, preferred_element_type=jnp.float32
    ) / math.sqrt(head_dim)
    raised = jnp.exp(scores) * key_mask.astype(jnp.float32)[:, None, None, :]
    probs = (raised / jnp.sum(raised, axis=-1, keepdims=True)).astype(jnp.bfloat16)
    mixed = jnp.einsum("bhqk,bkhd->bqhd", probs, value_rows, preferred_element_type=jnp.float32)
    mixed = mixed.astype(jnp.bfloat16).reshape(series_count * seq_length, half_width)
    update = jnp.dot(mixed, output_weight, preferred_element_type=jnp.float32)
    return (input_wide + update.reshape(series_count, seq_length, model_width)).astype(jnp.bfloat16)


def on_device(history, keymask, codes, plan_table, query_weights, output_weights, gains, cotangent):
    section_index = lax.axis_index("section")
    section_count = lax.axis_size("section")
    half_sections = section_count // 2
    micro_count, series_count, seq_length, model_width = history.shape
    rows = micro_count * series_count
    act_shape = (rows, seq_length, model_width)
    fsdp_count = lax.axis_size("fsdp")
    if fsdp_count & (fsdp_count - 1):
        query_weight = lax.all_gather(query_weights, "fsdp", axis=1, tiled=True)[0]
        output_weight = lax.all_gather(output_weights, "fsdp", axis=1, tiled=True)[0]
    else:
        query_weight, output_weight = butterfly_gathers(
            [query_weights, output_weights], exchange_orders(fsdp_count), "fsdp", fsdp_count
        )
    gain_vector = gains[0]
    code_rows = codes.reshape(micro_count, series_count, seq_length)
    code_count = plan_table.shape[0]
    one_hot = (code_rows[..., None] == jnp.arange(code_count, dtype=jnp.int32)).astype(jnp.bfloat16)
    plan_tokens = jnp.einsum(
        "msln,nd->msld", one_hot, plan_table, preferred_element_type=jnp.float32
    ).astype(jnp.bfloat16).reshape(act_shape)
    key_mask = keymask.reshape(rows, seq_length)
    history_rows = history.reshape(act_shape)

    def encoder_map(layer_input, layer_gain):
        return attend_layer(
            layer_input, layer_input, key_mask, query_weight, output_weight, layer_gain
        )

    def decoder_map(layer_input, layer_memory, layer_gain):
        return attend_layer(
            layer_input, layer_memory, key_mask, query_weight, output_weight, layer_gain
        )

    saved_inputs = {}
    got_input = None
    got_memory = None
    for tick in range(section_count - 1):
        if tick == 0:
            layer_input = history_rows
        elif tick == half_sections:
            layer_input = plan_tokens
        else:
            layer_input = got_input
        if tick < half_sections:
            output = encoder_map(layer_input, gain_vector)
            saved_inputs[tick] = (layer_input, None)
            if tick == half_sections - 1:
                got_memory = send_to(output, "section", tick, tick + 1)
            else:
                got_input = send_to(output, "section", tick, tick + 1)
        else:
            output = decoder_map(layer_input, got_memory, gain_vector)
            saved_inputs[tick] = (layer_input, got_memory)
            got_input, got_memory = send_to((output, got_memory), "section", tick, tick + 1)
    last = section_count - 1
    if last == half_sections:
        saved_inputs[last] = (plan_tokens, got_memory)
    else:
        saved_inputs[last] = (got_input, got_memory)

    zero_gain = jnp.zeros_like(gain_vector)
    grads_out = jnp.zeros(act_shape, jnp.bfloat16)
    gain_total = zero_gain
    got_grad = None
    got_memory_grad = None
    for tick in range(section_count):
        run = section_count - 1 - tick
        out_grad = cotangent.reshape(act_shape) if run == section_count - 1 else got_grad
        layer_input, layer_memory = saved_inputs[run]
        mine = section_index == run
        if run >= half_sections:
            _, pull = jax.vjp(decoder_map, layer_input, layer_memory, gain_vector)
            input_grad, memory_grad, gain_grad = pull(out_grad)
            if got_memory_grad is not None:
                memory_grad = got_memory_grad + memory_grad
            if run == half_sections:
                got_grad = send_to(memory_grad, "section", run, run - 1)
            else:
                got_grad, got_memory_grad = send_to(
                    (input_grad, memory_grad), "section", run, run - 1
                )
        else:
            _, pull = jax.vjp(encoder_map, layer_input, gain_vector)
            input_grad, gain_grad = pull(out_grad)
            if run > 0:
                got_grad = send_to(input_grad, "section", run, run - 1)
        grads_out = jnp.where(mine, input_grad, grads_out)
        gain_total = gain_total + jnp.where(mine, gain_grad, zero_gain)
    gain_total = butterfly_sum(gain_total, "fsdp", fsdp_count)
    grads_out = grads_out.reshape(history.shape)
    return (grads_out[None], gain_total[None])


def solution(mesh):
    return jax.shard_map(
        on_device,
        mesh=mesh,
        in_specs=(
            P(None, "fsdp", None, None),
            P(None, "fsdp", None),
            P(None, "fsdp", None, None),
            P(),
            P("section", "fsdp", None),
            P("section", "fsdp", None),
            P("section", None),
            P(None, "fsdp", None, None),
        ),
        out_specs=(P("section", None, "fsdp", None, None), P("section", None)),
        check_vma=False,
    )
```

```python
import math

import jax
import jax.numpy as jnp
from jax import lax
from jax.sharding import PartitionSpec as P

HEADS = 8


EPSILON = 1e-05


def send_to(arrays, axis, source, target):
    return lax.ppermute(arrays, axis, [(source, target)])


def exchange_orders(size):
    steps = []
    step = size // 2
    while step >= 1:
        steps.append(step)
        step //= 2
    other = list(steps)
    if len(other) >= 3:
        other[1], other[2] = other[2], other[1]
    return steps, other


def butterfly_gathers(shards, orders, axis, size):
    index = lax.axis_index(axis)
    held = [shard for shard in shards]
    done = [[] for _ in shards]
    for level in range(len(orders[0])):
        for which, order in enumerate(orders):
            step = order[level]
            other = lax.ppermute(held[which], axis, [(j, j ^ step) for j in range(size)])
            upper = ((index // step) % 2) == 1
            low = jnp.where(upper, other, held[which])
            high = jnp.where(upper, held[which], other)
            grid = (2,) * len(done[which]) + held[which].shape[1:]
            place = sum(1 for value in done[which] if value > step)
            held[which] = jnp.stack(
                [low.reshape(grid), high.reshape(grid)], axis=place
            ).reshape((-1,) + held[which].shape[1:])
            done[which].append(step)
    return [array.reshape(-1, array.shape[-1]) for array in held]


def butterfly_sum(value, axis, size):
    if size & (size - 1):
        return lax.psum(value, axis)
    step = 1
    while step < size:
        value = value + lax.ppermute(value, axis, [(j, j ^ step) for j in range(size)])
        step *= 2
    return value


def rms_scale(inputs, gain_vector):
    return (
        inputs
        * lax.rsqrt(jnp.mean(inputs * inputs, axis=-1, keepdims=True) + EPSILON)
        * gain_vector
    )


def attend_layer(section_input, source, key_mask, query_weight, output_weight, gain_vector):
    series_count, seq_length, model_width = section_input.shape
    half_width = model_width // 2
    head_dim = half_width // HEADS
    head_shape = (series_count, seq_length, HEADS, head_dim)
    input_wide = section_input.astype(jnp.float32)
    normed = rms_scale(input_wide, gain_vector)
    normed_source = rms_scale(source.astype(jnp.float32), gain_vector)
    normed_rows = normed.astype(jnp.bfloat16).reshape(series_count * seq_length, model_width)
    query_flat = jnp.dot(normed_rows, query_weight, preferred_element_type=jnp.float32)
    queries = query_flat.astype(jnp.bfloat16).reshape(head_shape)
    key_rows = normed_source[..., :half_width].astype(jnp.bfloat16).reshape(head_shape)
    value_rows = normed_source[..., half_width:].astype(jnp.bfloat16).reshape(head_shape)
    scores = jnp.einsum(
        "bqhd,bkhd->bhqk", queries, key_rows, preferred_element_type=jnp.float32
    ) / math.sqrt(head_dim)
    raised = jnp.exp(scores) * key_mask.astype(jnp.float32)[:, None, None, :]
    probs = (raised / jnp.sum(raised, axis=-1, keepdims=True)).astype(jnp.bfloat16)
    mixed = jnp.einsum("bhqk,bkhd->bqhd", probs, value_rows, preferred_element_type=jnp.float32)
    mixed = mixed.astype(jnp.bfloat16).reshape(series_count * seq_length, half_width)
    update = jnp.dot(mixed, output_weight, preferred_element_type=jnp.float32)
    return (input_wide + update.reshape(series_count, seq_length, model_width)).astype(jnp.bfloat16)


def on_device(history, keymask, codes, plan_table, query_weights, output_weights, gains, cotangent):
    section_index = lax.axis_index("section")
    section_count = lax.axis_size("section")
    half_sections = section_count // 2
    micro_count, series_count, seq_length, model_width = history.shape
    rows = micro_count * series_count
    act_shape = (rows, seq_length, model_width)
    fsdp_count = lax.axis_size("fsdp")
    if fsdp_count & (fsdp_count - 1):
        query_weight = lax.all_gather(query_weights, "fsdp", axis=1, tiled=True)[0]
        output_weight = lax.all_gather(output_weights, "fsdp", axis=1, tiled=True)[0]
    else:
        query_weight, output_weight = butterfly_gathers(
            [query_weights, output_weights], exchange_orders(fsdp_count), "fsdp", fsdp_count
        )
    gain_vector = gains[0]
    code_rows = codes.reshape(micro_count, series_count, seq_length)
    code_count = plan_table.shape[0]
    one_hot = (code_rows[..., None] == jnp.arange(code_count, dtype=jnp.int32)).astype(jnp.bfloat16)
    plan_tokens = jnp.einsum(
        "msln,nd->msld", one_hot, plan_table, preferred_element_type=jnp.float32
    ).astype(jnp.bfloat16).reshape(act_shape)
    key_mask = keymask.reshape(rows, seq_length)
    history_rows = history.reshape(act_shape)

    def encoder_map(layer_input, layer_gain):
        return attend_layer(
            layer_input, layer_input, key_mask, query_weight, output_weight, layer_gain
        )

    def decoder_map(layer_input, layer_memory, layer_gain):
        return attend_layer(
            layer_input, layer_memory, key_mask, query_weight, output_weight, layer_gain
        )

    saved_inputs = {}
    got_input = None
    got_memory = None
    for tick in range(section_count - 1):
        if tick == 0:
            layer_input = history_rows
        elif tick == half_sections:
            layer_input = plan_tokens
        else:
            layer_input = got_input
        if tick < half_sections:
            output = encoder_map(layer_input, gain_vector)
            saved_inputs[tick] = (layer_input, None)
            if tick == half_sections - 1:
                got_memory = send_to(output, "section", tick, tick + 1)
            else:
                got_input = send_to(output, "section", tick, tick + 1)
        else:
            output = decoder_map(layer_input, got_memory, gain_vector)
            saved_inputs[tick] = (layer_input, got_memory)
            got_input, got_memory = send_to((output, got_memory), "section", tick, tick + 1)
    last = section_count - 1
    if last == half_sections:
        saved_inputs[last] = (plan_tokens, got_memory)
    else:
        saved_inputs[last] = (got_input, got_memory)

    zero_gain = jnp.zeros_like(gain_vector)
    grads_out = jnp.zeros(act_shape, jnp.bfloat16)
    gain_total = zero_gain
    got_grad = None
    got_memory_grad = None
    for tick in range(section_count):
        run = section_count - 1 - tick
        out_grad = cotangent.reshape(act_shape) if run == section_count - 1 else got_grad
        layer_input, layer_memory = saved_inputs[run]
        mine = section_index == run
        if run >= half_sections:
            _, pull = jax.vjp(decoder_map, layer_input, layer_memory, gain_vector)
            input_grad, memory_grad, gain_grad = pull(out_grad)
            if got_memory_grad is not None:
                memory_grad = got_memory_grad + memory_grad
            if run == half_sections:
                got_grad = send_to(memory_grad, "section", run, run - 1)
            else:
                got_grad, got_memory_grad = send_to(
                    (input_grad, memory_grad), "section", run, run - 1
                )
        else:
            _, pull = jax.vjp(encoder_map, layer_input, gain_vector)
            input_grad, gain_grad = pull(out_grad)
            if run > 0:
                got_grad = send_to(input_grad, "section", run, run - 1)
        grads_out = jnp.where(mine, input_grad, grads_out)
        gain_total = gain_total + jnp.where(mine, gain_grad, zero_gain)
    gain_total = butterfly_sum(gain_total, "fsdp", fsdp_count)
    grads_out = grads_out.reshape(history.shape)
    return (grads_out[None], gain_total[None])


def solution(mesh):
    return jax.shard_map(
        on_device,
        mesh=mesh,
        in_specs=(
            P(None, "fsdp", None, None),
            P(None, "fsdp", None),
            P(None, "fsdp", None, None),
            P(),
            P("section", "fsdp", None),
            P("section", "fsdp", None),
            P("section", None),
            P(None, "fsdp", None, None),
        ),
        out_specs=(P("section", None, "fsdp", None, None), P("section", None)),
        check_vma=False,
    )
```

```python
import math

import jax
import jax.numpy as jnp
from jax import lax
from jax.sharding import PartitionSpec as P

HEADS = 8


EPSILON = 1e-05


def send_to(arrays, axis, source, target):
    return lax.ppermute(arrays, axis, [(source, target)])


def exchange_orders(size):
    steps = []
    step = size // 2
    while step >= 1:
        steps.append(step)
        step //= 2
    other = list(steps)
    if len(other) >= 3:
        other[1], other[2] = other[2], other[1]
    return other, steps


def butterfly_gathers(shards, orders, axis, size):
    index = lax.axis_index(axis)
    held = [shard for shard in shards]
    done = [[] for _ in shards]
    for level in range(len(orders[0])):
        for which, order in enumerate(orders):
            step = order[level]
            other = lax.ppermute(held[which], axis, [(j, j ^ step) for j in range(size)])
            upper = ((index // step) % 2) == 1
            low = jnp.where(upper, other, held[which])
            high = jnp.where(upper, held[which], other)
            grid = (2,) * len(done[which]) + held[which].shape[1:]
            place = sum(1 for value in done[which] if value > step)
            held[which] = jnp.stack(
                [low.reshape(grid), high.reshape(grid)], axis=place
            ).reshape((-1,) + held[which].shape[1:])
            done[which].append(step)
    return [array.reshape(-1, array.shape[-1]) for array in held]


def butterfly_sum(value, axis, size):
    if size & (size - 1):
        return lax.psum(value, axis)
    step = 1
    while step < size:
        value = value + lax.ppermute(value, axis, [(j, j ^ step) for j in range(size)])
        step *= 2
    return value


def rms_scale(inputs, gain_vector):
    return (
        inputs
        * lax.rsqrt(jnp.mean(inputs * inputs, axis=-1, keepdims=True) + EPSILON)
        * gain_vector
    )


def attend_layer(section_input, source, key_mask, query_weight, output_weight, gain_vector):
    series_count, seq_length, model_width = section_input.shape
    half_width = model_width // 2
    head_dim = half_width // HEADS
    head_shape = (series_count, seq_length, HEADS, head_dim)
    input_wide = section_input.astype(jnp.float32)
    normed = rms_scale(input_wide, gain_vector)
    normed_source = rms_scale(source.astype(jnp.float32), gain_vector)
    normed_rows = normed.astype(jnp.bfloat16).reshape(series_count * seq_length, model_width)
    query_flat = jnp.dot(normed_rows, query_weight, preferred_element_type=jnp.float32)
    queries = query_flat.astype(jnp.bfloat16).reshape(head_shape)
    key_rows = normed_source[..., :half_width].astype(jnp.bfloat16).reshape(head_shape)
    value_rows = normed_source[..., half_width:].astype(jnp.bfloat16).reshape(head_shape)
    scores = jnp.einsum(
        "bqhd,bkhd->bhqk", queries, key_rows, preferred_element_type=jnp.float32
    ) / math.sqrt(head_dim)
    raised = jnp.exp(scores) * key_mask.astype(jnp.float32)[:, None, None, :]
    probs = (raised / jnp.sum(raised, axis=-1, keepdims=True)).astype(jnp.bfloat16)
    mixed = jnp.einsum("bhqk,bkhd->bqhd", probs, value_rows, preferred_element_type=jnp.float32)
    mixed = mixed.astype(jnp.bfloat16).reshape(series_count * seq_length, half_width)
    update = jnp.dot(mixed, output_weight, preferred_element_type=jnp.float32)
    return (input_wide + update.reshape(series_count, seq_length, model_width)).astype(jnp.bfloat16)


def on_device(history, keymask, codes, plan_table, query_weights, output_weights, gains, cotangent):
    section_index = lax.axis_index("section")
    section_count = lax.axis_size("section")
    half_sections = section_count // 2
    micro_count, series_count, seq_length, model_width = history.shape
    rows = micro_count * series_count
    act_shape = (rows, seq_length, model_width)
    fsdp_count = lax.axis_size("fsdp")
    if fsdp_count & (fsdp_count - 1):
        query_weight = lax.all_gather(query_weights, "fsdp", axis=1, tiled=True)[0]
        output_weight = lax.all_gather(output_weights, "fsdp", axis=1, tiled=True)[0]
    else:
        query_weight, output_weight = butterfly_gathers(
            [query_weights, output_weights], exchange_orders(fsdp_count), "fsdp", fsdp_count
        )
    gain_vector = gains[0]
    code_rows = codes.reshape(micro_count, series_count, seq_length)
    code_count = plan_table.shape[0]
    one_hot = (code_rows[..., None] == jnp.arange(code_count, dtype=jnp.int32)).astype(jnp.bfloat16)
    plan_tokens = jnp.einsum(
        "msln,nd->msld", one_hot, plan_table, preferred_element_type=jnp.float32
    ).astype(jnp.bfloat16).reshape(act_shape)
    key_mask = keymask.reshape(rows, seq_length)
    history_rows = history.reshape(act_shape)

    def encoder_map(layer_input, layer_gain):
        return attend_layer(
            layer_input, layer_input, key_mask, query_weight, output_weight, layer_gain
        )

    def decoder_map(layer_input, layer_memory, layer_gain):
        return attend_layer(
            layer_input, layer_memory, key_mask, query_weight, output_weight, layer_gain
        )

    saved_inputs = {}
    got_input = None
    got_memory = None
    for tick in range(section_count - 1):
        if tick == 0:
            layer_input = history_rows
        elif tick == half_sections:
            layer_input = plan_tokens
        else:
            layer_input = got_input
        if tick < half_sections:
            output = encoder_map(layer_input, gain_vector)
            saved_inputs[tick] = (layer_input, None)
            if tick == half_sections - 1:
                got_memory = send_to(output, "section", tick, tick + 1)
            else:
                got_input = send_to(output, "section", tick, tick + 1)
        else:
            output = decoder_map(layer_input, got_memory, gain_vector)
            saved_inputs[tick] = (layer_input, got_memory)
            got_input, got_memory = send_to((output, got_memory), "section", tick, tick + 1)
    last = section_count - 1
    if last == half_sections:
        saved_inputs[last] = (plan_tokens, got_memory)
    else:
        saved_inputs[last] = (got_input, got_memory)

    zero_gain = jnp.zeros_like(gain_vector)
    grads_out = jnp.zeros(act_shape, jnp.bfloat16)
    gain_total = zero_gain
    got_grad = None
    got_memory_grad = None
    for tick in range(section_count):
        run = section_count - 1 - tick
        out_grad = cotangent.reshape(act_shape) if run == section_count - 1 else got_grad
        layer_input, layer_memory = saved_inputs[run]
        mine = section_index == run
        if run >= half_sections:
            _, pull = jax.vjp(decoder_map, layer_input, layer_memory, gain_vector)
            input_grad, memory_grad, gain_grad = pull(out_grad)
            if got_memory_grad is not None:
                memory_grad = got_memory_grad + memory_grad
            if run == half_sections:
                got_grad = send_to(memory_grad, "section", run, run - 1)
            else:
                got_grad, got_memory_grad = send_to(
                    (input_grad, memory_grad), "section", run, run - 1
                )
        else:
            _, pull = jax.vjp(encoder_map, layer_input, gain_vector)
            input_grad, gain_grad = pull(out_grad)
            if run > 0:
                got_grad = send_to(input_grad, "section", run, run - 1)
        grads_out = jnp.where(mine, input_grad, grads_out)
        gain_total = gain_total + jnp.where(mine, gain_grad, zero_gain)
    gain_total = butterfly_sum(gain_total, "fsdp", fsdp_count)
    grads_out = grads_out.reshape(history.shape)
    return (grads_out[None], gain_total[None])


def solution(mesh):
    return jax.shard_map(
        on_device,
        mesh=mesh,
        in_specs=(
            P(None, "fsdp", None, None),
            P(None, "fsdp", None),
            P(None, "fsdp", None, None),
            P(),
            P("section", "fsdp", None),
            P("section", "fsdp", None),
            P("section", None),
            P(None, "fsdp", None, None),
        ),
        out_specs=(P("section", None, "fsdp", None, None), P("section", None)),
        check_vma=False,
    )
```

```python
import math

import jax
import jax.numpy as jnp
from jax import lax
from jax.sharding import PartitionSpec as P

HEADS = 8


EPSILON = 1e-05


def send_to(arrays, axis, source, target):
    def halves(array):
        half = array.shape[0] // 2
        if half == 0:
            return (array,)
        return (array[:half], array[half:])

    leaves, tree = jax.tree.flatten(arrays)
    parts = [halves(leaf) for leaf in leaves]
    moved = lax.ppermute(tuple(piece for pieces in parts for piece in pieces), axis, [(source, target)])
    joined = []
    at = 0
    for pieces in parts:
        joined.append(jnp.concatenate(moved[at:at + len(pieces)], axis=0))
        at += len(pieces)
    return jax.tree.unflatten(tree, joined)


def exchange_orders(size):
    steps = []
    step = size // 2
    while step >= 1:
        steps.append(step)
        step //= 2
    other = list(steps)
    if len(other) >= 3:
        other[1], other[2] = other[2], other[1]
    return other, steps


def butterfly_gathers(shards, orders, axis, size):
    index = lax.axis_index(axis)
    held = [shard for shard in shards]
    done = [[] for _ in shards]
    for level in range(len(orders[0])):
        for which, order in enumerate(orders):
            step = order[level]
            other = lax.ppermute(held[which], axis, [(j, j ^ step) for j in range(size)])
            upper = ((index // step) % 2) == 1
            low = jnp.where(upper, other, held[which])
            high = jnp.where(upper, held[which], other)
            grid = (2,) * len(done[which]) + held[which].shape[1:]
            place = sum(1 for value in done[which] if value > step)
            held[which] = jnp.stack(
                [low.reshape(grid), high.reshape(grid)], axis=place
            ).reshape((-1,) + held[which].shape[1:])
            done[which].append(step)
    return [array.reshape(-1, array.shape[-1]) for array in held]


def butterfly_sum(value, axis, size):
    if size & (size - 1):
        return lax.psum(value, axis)
    step = 1
    while step < size:
        value = value + lax.ppermute(value, axis, [(j, j ^ step) for j in range(size)])
        step *= 2
    return value


def rms_scale(inputs, gain_vector):
    return (
        inputs
        * lax.rsqrt(jnp.mean(inputs * inputs, axis=-1, keepdims=True) + EPSILON)
        * gain_vector
    )


def attend_layer(section_input, source, key_mask, query_weight, output_weight, gain_vector):
    series_count, seq_length, model_width = section_input.shape
    half_width = model_width // 2
    head_dim = half_width // HEADS
    head_shape = (series_count, seq_length, HEADS, head_dim)
    input_wide = section_input.astype(jnp.float32)
    normed = rms_scale(input_wide, gain_vector)
    normed_source = rms_scale(source.astype(jnp.float32), gain_vector)
    normed_rows = normed.astype(jnp.bfloat16).reshape(series_count * seq_length, model_width)
    query_flat = jnp.dot(normed_rows, query_weight, preferred_element_type=jnp.float32)
    queries = query_flat.astype(jnp.bfloat16).reshape(head_shape)
    key_rows = normed_source[..., :half_width].astype(jnp.bfloat16).reshape(head_shape)
    value_rows = normed_source[..., half_width:].astype(jnp.bfloat16).reshape(head_shape)
    scores = jnp.einsum(
        "bqhd,bkhd->bhqk", queries, key_rows, preferred_element_type=jnp.float32
    ) / math.sqrt(head_dim)
    raised = jnp.exp(scores) * key_mask.astype(jnp.float32)[:, None, None, :]
    probs = (raised / jnp.sum(raised, axis=-1, keepdims=True)).astype(jnp.bfloat16)
    mixed = jnp.einsum("bhqk,bkhd->bqhd", probs, value_rows, preferred_element_type=jnp.float32)
    mixed = mixed.astype(jnp.bfloat16).reshape(series_count * seq_length, half_width)
    update = jnp.dot(mixed, output_weight, preferred_element_type=jnp.float32)
    return (input_wide + update.reshape(series_count, seq_length, model_width)).astype(jnp.bfloat16)


def on_device(history, keymask, codes, plan_table, query_weights, output_weights, gains, cotangent):
    section_index = lax.axis_index("section")
    section_count = lax.axis_size("section")
    half_sections = section_count // 2
    micro_count, series_count, seq_length, model_width = history.shape
    rows = micro_count * series_count
    act_shape = (rows, seq_length, model_width)
    fsdp_count = lax.axis_size("fsdp")
    if fsdp_count & (fsdp_count - 1):
        query_weight = lax.all_gather(query_weights, "fsdp", axis=1, tiled=True)[0]
        output_weight = lax.all_gather(output_weights, "fsdp", axis=1, tiled=True)[0]
    else:
        query_weight, output_weight = butterfly_gathers(
            [query_weights, output_weights], exchange_orders(fsdp_count), "fsdp", fsdp_count
        )
    gain_vector = gains[0]
    code_rows = codes.reshape(micro_count, series_count, seq_length)
    code_count = plan_table.shape[0]
    one_hot = (code_rows[..., None] == jnp.arange(code_count, dtype=jnp.int32)).astype(jnp.bfloat16)
    plan_tokens = jnp.einsum(
        "msln,nd->msld", one_hot, plan_table, preferred_element_type=jnp.float32
    ).astype(jnp.bfloat16).reshape(act_shape)
    key_mask = keymask.reshape(rows, seq_length)
    history_rows = history.reshape(act_shape)

    def encoder_map(layer_input, layer_gain):
        return attend_layer(
            layer_input, layer_input, key_mask, query_weight, output_weight, layer_gain
        )

    def decoder_map(layer_input, layer_memory, layer_gain):
        return attend_layer(
            layer_input, layer_memory, key_mask, query_weight, output_weight, layer_gain
        )

    saved_inputs = {}
    got_input = None
    got_memory = None
    for tick in range(section_count - 1):
        if tick == 0:
            layer_input = history_rows
        elif tick == half_sections:
            layer_input = plan_tokens
        else:
            layer_input = got_input
        if tick < half_sections:
            output = encoder_map(layer_input, gain_vector)
            saved_inputs[tick] = (layer_input, None)
            if tick == half_sections - 1:
                got_memory = send_to(output, "section", tick, tick + 1)
            else:
                got_input = send_to(output, "section", tick, tick + 1)
        else:
            output = decoder_map(layer_input, got_memory, gain_vector)
            saved_inputs[tick] = (layer_input, got_memory)
            got_input, got_memory = send_to((output, got_memory), "section", tick, tick + 1)
    last = section_count - 1
    if last == half_sections:
        saved_inputs[last] = (plan_tokens, got_memory)
    else:
        saved_inputs[last] = (got_input, got_memory)

    zero_gain = jnp.zeros_like(gain_vector)
    grads_out = jnp.zeros(act_shape, jnp.bfloat16)
    gain_total = zero_gain
    got_grad = None
    got_memory_grad = None
    for tick in range(section_count):
        run = section_count - 1 - tick
        out_grad = cotangent.reshape(act_shape) if run == section_count - 1 else got_grad
        layer_input, layer_memory = saved_inputs[run]
        mine = section_index == run
        if run >= half_sections:
            _, pull = jax.vjp(decoder_map, layer_input, layer_memory, gain_vector)
            input_grad, memory_grad, gain_grad = pull(out_grad)
            if got_memory_grad is not None:
                memory_grad = got_memory_grad + memory_grad
            if run == half_sections:
                got_grad = send_to(memory_grad, "section", run, run - 1)
            else:
                got_grad, got_memory_grad = send_to(
                    (input_grad, memory_grad), "section", run, run - 1
                )
        else:
            _, pull = jax.vjp(encoder_map, layer_input, gain_vector)
            input_grad, gain_grad = pull(out_grad)
            if run > 0:
                got_grad = send_to(input_grad, "section", run, run - 1)
        grads_out = jnp.where(mine, input_grad, grads_out)
        gain_total = gain_total + jnp.where(mine, gain_grad, zero_gain)
    gain_total = butterfly_sum(gain_total, "fsdp", fsdp_count)
    grads_out = grads_out.reshape(history.shape)
    return (grads_out[None], gain_total[None])


def solution(mesh):
    return jax.shard_map(
        on_device,
        mesh=mesh,
        in_specs=(
            P(None, "fsdp", None, None),
            P(None, "fsdp", None),
            P(None, "fsdp", None, None),
            P(),
            P("section", "fsdp", None),
            P("section", "fsdp", None),
            P("section", None),
            P(None, "fsdp", None, None),
        ),
        out_specs=(P("section", None, "fsdp", None, None), P("section", None)),
        check_vma=False,
    )
```

```python
import math

import jax
import jax.numpy as jnp
from jax import lax
from jax.sharding import PartitionSpec as P

HEADS = 8


EPSILON = 1e-05


def send_to(arrays, axis, source, target):
    return lax.ppermute(arrays, axis, [(source, target)])


def exchange_orders(size):
    steps = []
    step = size // 2
    while step >= 1:
        steps.append(step)
        step //= 2
    other = list(steps)
    if len(other) >= 3:
        other[1], other[2] = other[2], other[1]
    return other, steps


def butterfly_gathers(shards, orders, axis, size):
    index = lax.axis_index(axis)
    held = [shard for shard in shards]
    done = [[] for _ in shards]
    for level in range(len(orders[0])):
        for which, order in enumerate(orders):
            step = order[level]
            other = lax.ppermute(held[which], axis, [(j, j ^ step) for j in range(size)])
            upper = ((index // step) % 2) == 1
            low = jnp.where(upper, other, held[which])
            high = jnp.where(upper, held[which], other)
            grid = (2,) * len(done[which]) + held[which].shape[1:]
            place = sum(1 for value in done[which] if value > step)
            held[which] = jnp.stack(
                [low.reshape(grid), high.reshape(grid)], axis=place
            ).reshape((-1,) + held[which].shape[1:])
            done[which].append(step)
    return [array.reshape(-1, array.shape[-1]) for array in held]


def butterfly_sum(value, axis, size):
    if size & (size - 1):
        return lax.psum(value, axis)
    step = 1
    while step < size:
        value = value + lax.ppermute(value, axis, [(j, j ^ step) for j in range(size)])
        step *= 2
    return value


def rms_scale(inputs, gain_vector):
    return (
        inputs
        * lax.rsqrt(jnp.mean(inputs * inputs, axis=-1, keepdims=True) + EPSILON)
        * gain_vector
    )


def attend_layer(section_input, source, key_mask, query_weight, output_weight, gain_vector):
    series_count, seq_length, model_width = section_input.shape
    half_width = model_width // 2
    head_dim = half_width // HEADS
    head_shape = (series_count, seq_length, HEADS, head_dim)
    input_wide = section_input.astype(jnp.float32)
    normed = rms_scale(input_wide, gain_vector)
    normed_source = rms_scale(source.astype(jnp.float32), gain_vector)
    normed_rows = normed.astype(jnp.bfloat16).reshape(series_count * seq_length, model_width)
    query_flat = jnp.dot(normed_rows, query_weight, preferred_element_type=jnp.float32)
    queries = query_flat.astype(jnp.bfloat16).reshape(head_shape)
    key_rows = normed_source[..., :half_width].astype(jnp.bfloat16).reshape(head_shape)
    value_rows = normed_source[..., half_width:].astype(jnp.bfloat16).reshape(head_shape)
    scores = jnp.einsum(
        "bqhd,bkhd->bhqk", queries, key_rows, preferred_element_type=jnp.float32
    ) / math.sqrt(head_dim)
    raised = jnp.exp(scores) * key_mask.astype(jnp.float32)[:, None, None, :]
    probs = (raised / jnp.sum(raised, axis=-1, keepdims=True)).astype(jnp.bfloat16)
    mixed = jnp.einsum("bhqk,bkhd->bqhd", probs, value_rows, preferred_element_type=jnp.float32)
    mixed = mixed.astype(jnp.bfloat16).reshape(series_count * seq_length, half_width)
    update = jnp.dot(mixed, output_weight, preferred_element_type=jnp.float32)
    return (input_wide + update.reshape(series_count, seq_length, model_width)).astype(jnp.bfloat16)


def on_device(history, keymask, codes, plan_table, query_weights, output_weights, gains, cotangent):
    section_index = lax.axis_index("section")
    section_count = lax.axis_size("section")
    half_sections = section_count // 2
    micro_count, series_count, seq_length, model_width = history.shape
    rows = micro_count * series_count
    act_shape = (rows, seq_length, model_width)
    fsdp_count = lax.axis_size("fsdp")
    if fsdp_count & (fsdp_count - 1):
        query_weight = lax.all_gather(query_weights, "fsdp", axis=1, tiled=True)[0]
        output_weight = lax.all_gather(output_weights, "fsdp", axis=1, tiled=True)[0]
    else:
        query_weight, output_weight = butterfly_gathers(
            [query_weights, output_weights], exchange_orders(fsdp_count), "fsdp", fsdp_count
        )
    gain_vector = gains[0]
    code_rows = codes.reshape(micro_count, series_count, seq_length)
    code_count = plan_table.shape[0]
    one_hot = (code_rows[..., None] == jnp.arange(code_count, dtype=jnp.int32)).astype(jnp.bfloat16)
    plan_tokens = jnp.einsum(
        "msln,nd->msld", one_hot, plan_table, preferred_element_type=jnp.float32
    ).astype(jnp.bfloat16).reshape(act_shape)
    key_mask = keymask.reshape(rows, seq_length)
    history_rows = history.reshape(act_shape)

    def encoder_map(layer_input, layer_gain):
        return attend_layer(
            layer_input, layer_input, key_mask, query_weight, output_weight, layer_gain
        )

    def decoder_map(layer_input, layer_memory, layer_gain):
        return attend_layer(
            layer_input, layer_memory, key_mask, query_weight, output_weight, layer_gain
        )

    saved_inputs = {}
    got_input = None
    got_memory = None
    for tick in range(section_count - 1):
        if tick == 0:
            layer_input = history_rows
        elif tick == half_sections:
            layer_input = plan_tokens
        else:
            layer_input = got_input
        if tick < half_sections:
            output, pull = jax.vjp(encoder_map, layer_input, gain_vector)
            saved_inputs[tick] = pull
            if tick == half_sections - 1:
                got_memory = send_to(output, "section", tick, tick + 1)
            else:
                got_input = send_to(output, "section", tick, tick + 1)
        else:
            output = decoder_map(layer_input, got_memory, gain_vector)
            saved_inputs[tick] = (layer_input, got_memory)
            got_input, got_memory = send_to((output, got_memory), "section", tick, tick + 1)
    last = section_count - 1
    if last == half_sections:
        saved_inputs[last] = (plan_tokens, got_memory)
    else:
        saved_inputs[last] = (got_input, got_memory)

    zero_gain = jnp.zeros_like(gain_vector)
    grads_out = jnp.zeros(act_shape, jnp.bfloat16)
    gain_total = zero_gain
    got_grad = None
    got_memory_grad = None
    for tick in range(section_count):
        run = section_count - 1 - tick
        out_grad = cotangent.reshape(act_shape) if run == section_count - 1 else got_grad
        mine = section_index == run
        if run >= half_sections:
            layer_input, layer_memory = saved_inputs[run]
            _, pull = jax.vjp(decoder_map, layer_input, layer_memory, gain_vector)
            input_grad, memory_grad, gain_grad = pull(out_grad)
            if got_memory_grad is not None:
                memory_grad = got_memory_grad + memory_grad
            if run == half_sections:
                got_grad = send_to(memory_grad, "section", run, run - 1)
            else:
                got_grad, got_memory_grad = send_to(
                    (input_grad, memory_grad), "section", run, run - 1
                )
        else:
            input_grad, gain_grad = saved_inputs[run](out_grad)
            if run > 0:
                got_grad = send_to(input_grad, "section", run, run - 1)
        grads_out = jnp.where(mine, input_grad, grads_out)
        gain_total = gain_total + jnp.where(mine, gain_grad, zero_gain)
    gain_total = butterfly_sum(gain_total, "fsdp", fsdp_count)
    grads_out = grads_out.reshape(history.shape)
    return (grads_out[None], gain_total[None])


def solution(mesh):
    return jax.shard_map(
        on_device,
        mesh=mesh,
        in_specs=(
            P(None, "fsdp", None, None),
            P(None, "fsdp", None),
            P(None, "fsdp", None, None),
            P(),
            P("section", "fsdp", None),
            P("section", "fsdp", None),
            P("section", None),
            P(None, "fsdp", None, None),
        ),
        out_specs=(P("section", None, "fsdp", None, None), P("section", None)),
        check_vma=False,
    )
```

```python
import math

import jax
import jax.numpy as jnp
from jax import lax
from jax.sharding import PartitionSpec as P

HEADS = 8


EPSILON = 1e-05


def send_to(arrays, axis, source, target):
    return lax.ppermute(arrays, axis, [(source, target)])


def exchange_orders(size):
    steps = []
    step = size // 2
    while step >= 1:
        steps.append(step)
        step //= 2
    other = list(steps)
    if len(other) >= 3:
        other[1], other[2] = other[2], other[1]
    return other, steps


def butterfly_gathers(shards, orders, axis, size):
    index = lax.axis_index(axis)
    held = [shard for shard in shards]
    done = [[] for _ in shards]
    for level in range(len(orders[0])):
        for which, order in enumerate(orders):
            step = order[level]
            other = lax.ppermute(held[which], axis, [(j, j ^ step) for j in range(size)])
            upper = ((index // step) % 2) == 1
            low = jnp.where(upper, other, held[which])
            high = jnp.where(upper, held[which], other)
            grid = (2,) * len(done[which]) + held[which].shape[1:]
            place = sum(1 for value in done[which] if value > step)
            held[which] = jnp.stack(
                [low.reshape(grid), high.reshape(grid)], axis=place
            ).reshape((-1,) + held[which].shape[1:])
            done[which].append(step)
    return [array.reshape(-1, array.shape[-1]) for array in held]


def butterfly_sum(value, axis, size):
    if size & (size - 1):
        return lax.psum(value, axis)
    step = 1
    while step < size:
        value = value + lax.ppermute(value, axis, [(j, j ^ step) for j in range(size)])
        step *= 2
    return value


def rms_scale(inputs, gain_vector):
    return (
        inputs
        * lax.rsqrt(jnp.mean(inputs * inputs, axis=-1, keepdims=True) + EPSILON)
        * gain_vector
    )


def attend_layer(section_input, source, key_mask, query_weight, output_weight, gain_vector):
    series_count, seq_length, model_width = section_input.shape
    half_width = model_width // 2
    head_dim = half_width // HEADS
    head_shape = (series_count, seq_length, HEADS, head_dim)
    input_wide = section_input.astype(jnp.float32)
    normed = rms_scale(input_wide, gain_vector)
    normed_source = rms_scale(source.astype(jnp.float32), gain_vector)
    normed_rows = normed.astype(jnp.bfloat16).reshape(series_count * seq_length, model_width)
    query_flat = jnp.dot(normed_rows, query_weight, preferred_element_type=jnp.float32)
    queries = query_flat.astype(jnp.bfloat16).reshape(head_shape)
    key_rows = normed_source[..., :half_width].astype(jnp.bfloat16).reshape(head_shape)
    value_rows = normed_source[..., half_width:].astype(jnp.bfloat16).reshape(head_shape)
    scores = jnp.einsum(
        "bqhd,bkhd->bhqk", queries, key_rows, preferred_element_type=jnp.float32
    ) / math.sqrt(head_dim)
    raised = jnp.exp(scores) * key_mask.astype(jnp.float32)[:, None, None, :]
    probs = (raised / jnp.sum(raised, axis=-1, keepdims=True)).astype(jnp.bfloat16)
    mixed = jnp.einsum("bhqk,bkhd->bqhd", probs, value_rows, preferred_element_type=jnp.float32)
    mixed = mixed.astype(jnp.bfloat16).reshape(series_count * seq_length, half_width)
    update = jnp.dot(mixed, output_weight, preferred_element_type=jnp.float32)
    return (input_wide + update.reshape(series_count, seq_length, model_width)).astype(jnp.bfloat16)


def two_section_relay(
    history_rows, plan_tokens, cotangent_rows, key_mask, query_weight, output_weight, gain_vector
):
    is_encoder = lax.axis_index("section") == 0
    half = history_rows.shape[0] // 2

    def part(array, which):
        return array[which * half:(which + 1) * half]

    def pick(encoder_value, decoder_value):
        return jnp.where(is_encoder, encoder_value, decoder_value)

    def layer_vjp(layer_input, layer_source, layer_mask, out_grad):
        def apply(x, source, layer_gain):
            return attend_layer(x, source, layer_mask, query_weight, output_weight, layer_gain)

        output, pull = jax.vjp(apply, layer_input, layer_source, gain_vector)
        return (output,) + pull(out_grad)

    both_ways = [(0, 1), (1, 0)]
    zero_gain = jnp.zeros_like(gain_vector)
    hist_a, hist_b = part(history_rows, 0), part(history_rows, 1)
    mask_a, mask_b = part(key_mask, 0), part(key_mask, 1)
    plan_a, plan_b = part(plan_tokens, 0), part(plan_tokens, 1)
    memory_a = attend_layer(hist_a, hist_a, mask_a, query_weight, output_weight, gain_vector)
    memory_a = send_to(memory_a, "section", 0, 1)
    memory_b, input_grad, memory_grad, gain_1 = layer_vjp(
        pick(hist_b, plan_a),
        pick(hist_b, memory_a),
        pick(mask_b, mask_a),
        pick(jnp.zeros_like(hist_b), part(cotangent_rows, 0)),
    )
    decoder_grad_a = input_grad
    received = lax.ppermute(pick(memory_b, memory_grad), "section", both_ways)
    _, input_grad, memory_grad, gain_2 = layer_vjp(
        pick(hist_a, plan_b),
        pick(hist_a, received),
        pick(mask_a, mask_b),
        pick(received, part(cotangent_rows, 1)),
    )
    encoder_grad_a = input_grad + memory_grad
    decoder_grad_b = input_grad
    memory_grad_b = send_to(memory_grad, "section", 1, 0)
    _, input_grad, memory_grad, gain_3 = layer_vjp(hist_b, hist_b, mask_b, memory_grad_b)
    encoder_grad_b = input_grad + memory_grad
    grads = jnp.concatenate(
        [pick(encoder_grad_a, decoder_grad_a), pick(encoder_grad_b, decoder_grad_b)], axis=0
    )
    gain_total = pick(zero_gain, gain_1) + gain_2 + pick(gain_3, zero_gain)
    return grads, gain_total


def on_device(history, keymask, codes, plan_table, query_weights, output_weights, gains, cotangent):
    section_index = lax.axis_index("section")
    section_count = lax.axis_size("section")
    half_sections = section_count // 2
    micro_count, series_count, seq_length, model_width = history.shape
    rows = micro_count * series_count
    act_shape = (rows, seq_length, model_width)
    fsdp_count = lax.axis_size("fsdp")
    if fsdp_count & (fsdp_count - 1):
        query_weight = lax.all_gather(query_weights, "fsdp", axis=1, tiled=True)[0]
        output_weight = lax.all_gather(output_weights, "fsdp", axis=1, tiled=True)[0]
    else:
        query_weight, output_weight = butterfly_gathers(
            [query_weights, output_weights], exchange_orders(fsdp_count), "fsdp", fsdp_count
        )
    gain_vector = gains[0]
    code_rows = codes.reshape(micro_count, series_count, seq_length)
    code_count = plan_table.shape[0]
    one_hot = (code_rows[..., None] == jnp.arange(code_count, dtype=jnp.int32)).astype(jnp.bfloat16)
    plan_tokens = jnp.einsum(
        "msln,nd->msld", one_hot, plan_table, preferred_element_type=jnp.float32
    ).astype(jnp.bfloat16).reshape(act_shape)
    key_mask = keymask.reshape(rows, seq_length)
    history_rows = history.reshape(act_shape)
    if section_count == 2 and micro_count % 2 == 0:
        grads_out, gain_total = two_section_relay(
            history_rows, plan_tokens, cotangent.reshape(act_shape), key_mask,
            query_weight, output_weight, gain_vector,
        )
        gain_total = butterfly_sum(gain_total, "fsdp", fsdp_count)
        return (grads_out.reshape(history.shape)[None], gain_total[None])

    def encoder_map(layer_input, layer_gain):
        return attend_layer(
            layer_input, layer_input, key_mask, query_weight, output_weight, layer_gain
        )

    def decoder_map(layer_input, layer_memory, layer_gain):
        return attend_layer(
            layer_input, layer_memory, key_mask, query_weight, output_weight, layer_gain
        )

    saved_inputs = {}
    got_input = None
    got_memory = None
    for tick in range(section_count - 1):
        if tick == 0:
            layer_input = history_rows
        elif tick == half_sections:
            layer_input = plan_tokens
        else:
            layer_input = got_input
        if tick < half_sections:
            output = encoder_map(layer_input, gain_vector)
            saved_inputs[tick] = (layer_input, None)
            if tick == half_sections - 1:
                got_memory = send_to(output, "section", tick, tick + 1)
            else:
                got_input = send_to(output, "section", tick, tick + 1)
        else:
            output = decoder_map(layer_input, got_memory, gain_vector)
            saved_inputs[tick] = (layer_input, got_memory)
            got_input, got_memory = send_to((output, got_memory), "section", tick, tick + 1)
    last = section_count - 1
    if last == half_sections:
        saved_inputs[last] = (plan_tokens, got_memory)
    else:
        saved_inputs[last] = (got_input, got_memory)

    zero_gain = jnp.zeros_like(gain_vector)
    grads_out = jnp.zeros(act_shape, jnp.bfloat16)
    gain_total = zero_gain
    got_grad = None
    got_memory_grad = None
    for tick in range(section_count):
        run = section_count - 1 - tick
        out_grad = cotangent.reshape(act_shape) if run == section_count - 1 else got_grad
        layer_input, layer_memory = saved_inputs[run]
        mine = section_index == run
        if run >= half_sections:
            _, pull = jax.vjp(decoder_map, layer_input, layer_memory, gain_vector)
            input_grad, memory_grad, gain_grad = pull(out_grad)
            if got_memory_grad is not None:
                memory_grad = got_memory_grad + memory_grad
            if run == half_sections:
                got_grad = send_to(memory_grad, "section", run, run - 1)
            else:
                got_grad, got_memory_grad = send_to(
                    (input_grad, memory_grad), "section", run, run - 1
                )
        else:
            _, pull = jax.vjp(encoder_map, layer_input, gain_vector)
            input_grad, gain_grad = pull(out_grad)
            if run > 0:
                got_grad = send_to(input_grad, "section", run, run - 1)
        grads_out = jnp.where(mine, input_grad, grads_out)
        gain_total = gain_total + jnp.where(mine, gain_grad, zero_gain)
    gain_total = butterfly_sum(gain_total, "fsdp", fsdp_count)
    grads_out = grads_out.reshape(history.shape)
    return (grads_out[None], gain_total[None])


def solution(mesh):
    return jax.shard_map(
        on_device,
        mesh=mesh,
        in_specs=(
            P(None, "fsdp", None, None),
            P(None, "fsdp", None),
            P(None, "fsdp", None, None),
            P(),
            P("section", "fsdp", None),
            P("section", "fsdp", None),
            P("section", None),
            P(None, "fsdp", None, None),
        ),
        out_specs=(P("section", None, "fsdp", None, None), P("section", None)),
        check_vma=False,
    )
```

```python
import math

import jax
import jax.numpy as jnp
from jax import lax
from jax.sharding import PartitionSpec as P

HEADS = 8


EPSILON = 1e-05


def send_to(arrays, axis, source, target):
    return lax.ppermute(arrays, axis, [(source, target)])


def exchange_orders(size):
    steps = []
    step = size // 2
    while step >= 1:
        steps.append(step)
        step //= 2
    other = list(steps)
    if len(other) >= 3:
        other[1], other[2] = other[2], other[1]
    return other, steps


def butterfly_gathers(shards, orders, axis, size):
    index = lax.axis_index(axis)
    held = [shard for shard in shards]
    done = [[] for _ in shards]
    for level in range(len(orders[0])):
        for which, order in enumerate(orders):
            step = order[level]
            other = lax.ppermute(held[which], axis, [(j, j ^ step) for j in range(size)])
            upper = ((index // step) % 2) == 1
            low = jnp.where(upper, other, held[which])
            high = jnp.where(upper, held[which], other)
            grid = (2,) * len(done[which]) + held[which].shape[1:]
            place = sum(1 for value in done[which] if value > step)
            held[which] = jnp.stack(
                [low.reshape(grid), high.reshape(grid)], axis=place
            ).reshape((-1,) + held[which].shape[1:])
            done[which].append(step)
    return [array.reshape(-1, array.shape[-1]) for array in held]


def butterfly_sum(value, axis, size):
    if size & (size - 1):
        return lax.psum(value, axis)
    index = lax.axis_index(axis)
    step = 1
    while step < size:
        width = 4 if step * 4 <= size else 2
        offsets = [step * k for k in range(1, width)]
        received = [value] + [
            lax.ppermute(value, axis, [(j, j ^ offset) for j in range(size)]) for offset in offsets
        ]
        own = (index // step) % width
        ordered = []
        for member in range(width):
            pick = received[0]
            for k in range(1, width):
                pick = jnp.where((own ^ member) == k, received[k], pick)
            ordered.append(pick)
        if width == 4:
            value = (ordered[0] + ordered[1]) + (ordered[2] + ordered[3])
        else:
            value = ordered[0] + ordered[1]
        step *= width
    return value


def rms_scale(inputs, gain_vector):
    return (
        inputs
        * lax.rsqrt(jnp.mean(inputs * inputs, axis=-1, keepdims=True) + EPSILON)
        * gain_vector
    )


def attend_layer(section_input, source, key_mask, query_weight, output_weight, gain_vector):
    series_count, seq_length, model_width = section_input.shape
    half_width = model_width // 2
    head_dim = half_width // HEADS
    head_shape = (series_count, seq_length, HEADS, head_dim)
    input_wide = section_input.astype(jnp.float32)
    normed = rms_scale(input_wide, gain_vector)
    normed_source = rms_scale(source.astype(jnp.float32), gain_vector)
    normed_rows = normed.astype(jnp.bfloat16).reshape(series_count * seq_length, model_width)
    query_flat = jnp.dot(normed_rows, query_weight, preferred_element_type=jnp.float32)
    queries = query_flat.astype(jnp.bfloat16).reshape(head_shape)
    key_rows = normed_source[..., :half_width].astype(jnp.bfloat16).reshape(head_shape)
    value_rows = normed_source[..., half_width:].astype(jnp.bfloat16).reshape(head_shape)
    scores = jnp.einsum(
        "bqhd,bkhd->bhqk", queries, key_rows, preferred_element_type=jnp.float32
    ) / math.sqrt(head_dim)
    raised = jnp.exp(scores) * key_mask.astype(jnp.float32)[:, None, None, :]
    probs = (raised / jnp.sum(raised, axis=-1, keepdims=True)).astype(jnp.bfloat16)
    mixed = jnp.einsum("bhqk,bkhd->bqhd", probs, value_rows, preferred_element_type=jnp.float32)
    mixed = mixed.astype(jnp.bfloat16).reshape(series_count * seq_length, half_width)
    update = jnp.dot(mixed, output_weight, preferred_element_type=jnp.float32)
    return (input_wide + update.reshape(series_count, seq_length, model_width)).astype(jnp.bfloat16)


def on_device(history, keymask, codes, plan_table, query_weights, output_weights, gains, cotangent):
    section_index = lax.axis_index("section")
    section_count = lax.axis_size("section")
    half_sections = section_count // 2
    micro_count, series_count, seq_length, model_width = history.shape
    rows = micro_count * series_count
    act_shape = (rows, seq_length, model_width)
    fsdp_count = lax.axis_size("fsdp")
    if fsdp_count & (fsdp_count - 1):
        query_weight = lax.all_gather(query_weights, "fsdp", axis=1, tiled=True)[0]
        output_weight = lax.all_gather(output_weights, "fsdp", axis=1, tiled=True)[0]
    else:
        query_weight, output_weight = butterfly_gathers(
            [query_weights, output_weights], exchange_orders(fsdp_count), "fsdp", fsdp_count
        )
    gain_vector = gains[0]
    code_rows = codes.reshape(micro_count, series_count, seq_length)
    code_count = plan_table.shape[0]
    one_hot = (code_rows[..., None] == jnp.arange(code_count, dtype=jnp.int32)).astype(jnp.bfloat16)
    plan_tokens = jnp.einsum(
        "msln,nd->msld", one_hot, plan_table, preferred_element_type=jnp.float32
    ).astype(jnp.bfloat16).reshape(act_shape)
    key_mask = keymask.reshape(rows, seq_length)
    history_rows = history.reshape(act_shape)

    def encoder_map(layer_input, layer_gain):
        return attend_layer(
            layer_input, layer_input, key_mask, query_weight, output_weight, layer_gain
        )

    def decoder_map(layer_input, layer_memory, layer_gain):
        return attend_layer(
            layer_input, layer_memory, key_mask, query_weight, output_weight, layer_gain
        )

    saved_inputs = {}
    got_input = None
    got_memory = None
    for tick in range(section_count - 1):
        if tick == 0:
            layer_input = history_rows
        elif tick == half_sections:
            layer_input = plan_tokens
        else:
            layer_input = got_input
        if tick < half_sections:
            output = encoder_map(layer_input, gain_vector)
            saved_inputs[tick] = (layer_input, None)
            if tick == half_sections - 1:
                got_memory = send_to(output, "section", tick, tick + 1)
            else:
                got_input = send_to(output, "section", tick, tick + 1)
        else:
            output = decoder_map(layer_input, got_memory, gain_vector)
            saved_inputs[tick] = (layer_input, got_memory)
            got_input, got_memory = send_to((output, got_memory), "section", tick, tick + 1)
    last = section_count - 1
    if last == half_sections:
        saved_inputs[last] = (plan_tokens, got_memory)
    else:
        saved_inputs[last] = (got_input, got_memory)

    zero_gain = jnp.zeros_like(gain_vector)
    grads_out = jnp.zeros(act_shape, jnp.bfloat16)
    gain_total = zero_gain
    got_grad = None
    got_memory_grad = None
    for tick in range(section_count):
        run = section_count - 1 - tick
        out_grad = cotangent.reshape(act_shape) if run == section_count - 1 else got_grad
        layer_input, layer_memory = saved_inputs[run]
        mine = section_index == run
        if run >= half_sections:
            _, pull = jax.vjp(decoder_map, layer_input, layer_memory, gain_vector)
            input_grad, memory_grad, gain_grad = pull(out_grad)
            if got_memory_grad is not None:
                memory_grad = got_memory_grad + memory_grad
            if run == half_sections:
                got_grad = send_to(memory_grad, "section", run, run - 1)
            else:
                got_grad, got_memory_grad = send_to(
                    (input_grad, memory_grad), "section", run, run - 1
                )
        else:
            _, pull = jax.vjp(encoder_map, layer_input, gain_vector)
            input_grad, gain_grad = pull(out_grad)
            if run > 0:
                got_grad = send_to(input_grad, "section", run, run - 1)
        grads_out = jnp.where(mine, input_grad, grads_out)
        gain_total = gain_total + jnp.where(mine, gain_grad, zero_gain)
    gain_total = butterfly_sum(gain_total, "fsdp", fsdp_count)
    grads_out = grads_out.reshape(history.shape)
    return (grads_out[None], gain_total[None])


def solution(mesh):
    return jax.shard_map(
        on_device,
        mesh=mesh,
        in_specs=(
            P(None, "fsdp", None, None),
            P(None, "fsdp", None),
            P(None, "fsdp", None, None),
            P(),
            P("section", "fsdp", None),
            P("section", "fsdp", None),
            P("section", None),
            P(None, "fsdp", None, None),
        ),
        out_specs=(P("section", None, "fsdp", None, None), P("section", None)),
        check_vma=False,
    )
```
